128 devices in a mesh: ctx: 16 (over y, z_hi, core), tp: 8 (over z_lo, x).
Axes of the slice: x: 4, y: 4, z: 4 (z_hi: 2, z_lo: 2; z = z_hi * 2 + z_lo), core: 2. Of those that a mesh axis runs over, the one named last changes fastest.
Arguments:
- queries: bfloat16 [32768, 8192], P('ctx', 'tp'), may hold values from -48 to 48
- keys: bfloat16 [32768, 1024], P(('ctx', 'tp')), may hold values from -6 to 6
- values: bfloat16 [32768, 1024], P(('ctx', 'tp')), may hold values from -6 to 6
- rope_factors: float32 [64], replicated, may hold values from 1 to 32
- doc_lengths: int32 [128], replicated, may hold values from 1 to 512, 32768 in all
- owner_map: int32 [16, 8], replicated, may hold values from 0 to 15, as said below
Outputs:
- attended: bfloat16 [32768, 8192], P('ctx', 'tp')
The draws below stay inside these ranges and needn't reach their ends.
Inputs may be any that keep to these rules, and one draw needn't show every extreme that they name: `owner_map`: row c lists the owners of the 8 blocks of index c: they are different devices, and every device owns exactly one block of each in-device number r, so exactly 8 blocks in all.
All inputs are finite; a program needn't handle non-finite values.
Results may differ from the reference program's by a relative error of at most 0.0051.
Values may be sent and summed in bfloat16 or wider, within the bound.
No kernel may reach another device: no remote copies, remote signals or barrier semaphores. Data moves between devices by JAX's collectives and lax.ppermute only.
A program may use at most 128 MiB of HBM per device.

```python
import math
import jax
import jax.numpy as jnp
import numpy as np
from jax import lax

HEADS = 64
KV = 8
HD = 128
BLOCKS_DEV = 8
TOKENS = 32768
NDOCS = 128
MAXDOC = 512
N_CTX = 16


def key_field(key):
    base = jax.random.fold_in(key, 11)
    return jnp.clip(jax.random.normal(base, (TOKENS, KV * HD), jnp.float32), -6.0, 6.0)


def draw_keys(key, part):
    return key_field(key).astype(jnp.bfloat16)


def draw_queries(key, part):
    base = jax.random.fold_in(key, 23)
    return jnp.clip(jax.random.normal(base, (TOKENS, HEADS * HD), jnp.float32), -6.0, 6.0).astype(jnp.bfloat16)


def draw_owner_map(key, part):
    first_key = jax.random.fold_in(key, 41)
    second_key = jax.random.fold_in(key, 43)
    third_key = jax.random.fold_in(key, 47)
    first_perm = jax.random.permutation(first_key, N_CTX)
    second_perm = jax.random.permutation(second_key, N_CTX)
    offsets = jax.random.permutation(third_key, N_CTX)[:BLOCKS_DEV]
    lookup = (first_perm[:, None] + offsets[None, :]) % N_CTX
    return second_perm[lookup].astype(jnp.int32)


def shard_levels(stream_key, dims, pieces, smallest, largest):
    def one(axis_at, parts):
        heights = jax.random.uniform(jax.random.fold_in(jax.random.fold_in(stream_key, 6), axis_at), (parts,), jnp.float32, smallest / len(pieces), largest / len(pieces))
        return jnp.repeat(jnp.exp(heights), dims[axis_at] // parts).reshape((-1,) + (1,) * (len(dims) - axis_at - 1))

    level = one(*pieces[0])
    for cut in pieces[1:]:
        level = level * one(*cut)
    return level


def length_profile(number_of, total, bound, skew):
    portions = [(1 << 20) // math.isqrt(standing ** skew) + 1 for standing in range(2, number_of + 1)]
    spare, given = total - bound - (number_of - 1), [1] * (number_of - 1)
    while spare > 0:
        free = [i for i in range(number_of - 1) if given[i] < bound]
        whole, budget = sum([portions[i] for i in free]), spare
        for i in free:
            addition = min(bound - given[i], max(1, budget * portions[i] // whole), spare)
            given[i] = given[i] + addition
            spare = spare - addition
    return np.array([bound] + given)


def ragged_sizes(key, count, total, most, slope):
    if count == 2:
        one = jax.random.randint(key, (), max(1, total - most), min(most, total - 1) + 1)
        return jnp.stack([one, total - one])
    sizes = jnp.asarray(length_profile(count, total, most, slope), jnp.int32)
    pairs = (count - 1) // 2
    source_of, taker = sizes[1:1 + 2 * pairs:2], sizes[2:2 + 2 * pairs:2]
    room = jnp.minimum(source_of - 1, most - taker)
    shifted = jax.random.randint(jax.random.fold_in(key, 1), (pairs,), 0, 1 << 20) % (room + 1)
    sizes = sizes.at[1:1 + 2 * pairs:2].set(source_of - shifted).at[2:2 + 2 * pairs:2].set(taker + shifted)
    return sizes[jax.random.permutation(jax.random.fold_in(key, 2), count)]


def bell_draw(own_key, shape, spread, bound, pieces=(), kind=jnp.bfloat16):
    gain = shard_levels(own_key, shape, pieces, -0.22, 0.18) if pieces else 1.0
    entries = jax.random.normal(own_key, shape, jnp.float32) * spread * gain
    return jnp.minimum(jnp.maximum(entries, -bound), bound).astype(kind)


def setup_inputs(seed: int = 0) -> dict:
    streams_of = jax.random.split(jax.random.key(seed), 7)
    return {
        "queries": draw_queries(jax.random.fold_in(streams_of[6], 71), 0),
        "keys": draw_keys(jax.random.fold_in(streams_of[6], 71), 0),
        "values": bell_draw(streams_of[2], (TOKENS, KV * HD), 1.0, 6.0, ((0, 128),)),
        "rope_factors": jnp.clip(jnp.exp(jax.random.uniform(streams_of[3], (HD // 2,), jnp.float32, math.log(1.0), math.log(32.0))), 1.0, 32.0),
        "doc_lengths": ragged_sizes(streams_of[4], NDOCS, TOKENS, MAXDOC, 2).astype(jnp.int32),
        "owner_map": draw_owner_map(jax.random.fold_in(streams_of[6], 71), 0),
    }


THETA = 500000.0

def doc_tables(lengths, positions):
    doc_ends = jnp.cumsum(lengths, dtype=jnp.int32)
    before = positions[:, None] >= doc_ends[None, :]
    doc_index = lax.optimization_barrier(jnp.sum(before.astype(jnp.int32), axis=1, dtype=jnp.int32))
    doc_start = lax.optimization_barrier(jnp.sum(jnp.where(before, lengths[None, :], 0), axis=1, dtype=jnp.int32))
    return (doc_index, positions - doc_start)

def rotate(vectors, offsets, factors):
    half_dim = vectors.shape[-1] // 2
    exponent = jnp.arange(half_dim, dtype=jnp.float32) * (2.0 / vectors.shape[-1])
    inverse = 1.0 / (factors * jnp.power(jnp.float32(THETA), exponent))
    angles = offsets.astype(jnp.float32)[:, None] * inverse[None, :]
    cosine = jnp.cos(angles)[:, None, :]
    sine_part = jnp.sin(angles)[:, None, :]
    first_half = vectors[..., :half_dim]
    second_half = vectors[..., half_dim:]
    return jnp.concatenate([first_half * cosine - second_half * sine_part, second_half * cosine + first_half * sine_part], axis=-1)

def source_table(owner_map):
    ctx_size = owner_map.shape[0]
    devices = jnp.arange(ctx_size, dtype=jnp.int32)
    matches = owner_map[None, :, :] == devices[:, None, None]
    return lax.optimization_barrier(jnp.sum(jnp.where(matches, devices[None, :, None], 0), axis=1, dtype=jnp.int32))

def slot_rows(sources_row, per_dev, block_rows):
    blocks = sources_row * per_dev + jnp.arange(per_dev, dtype=jnp.int32)
    return (blocks[:, None] * block_rows + jnp.arange(block_rows, dtype=jnp.int32)[None, :]).reshape(-1)

def reference(queries, keys, values, rope_factors, doc_lengths, owner_map):
    total_rows = queries.shape[0]
    ctx_size = owner_map.shape[0]
    per_dev = owner_map.shape[1]
    row_count = total_rows // ctx_size
    block_rows = row_count // per_dev
    pad_rows = row_count // 4
    span = pad_rows + block_rows
    head_dim = 2 * rope_factors.shape[0]
    heads_all = queries.shape[1] // head_dim
    kv_all = keys.shape[1] // head_dim
    group_size = heads_all // kv_all
    score_scale = 1.0 / math.sqrt(head_dim)
    positions = jnp.arange(total_rows, dtype=jnp.int32)
    doc_index, offsets = doc_tables(doc_lengths, positions)
    q_rot = rotate(queries.astype(jnp.float32).reshape(total_rows, heads_all, head_dim), offsets, rope_factors).astype(jnp.bfloat16)
    k_rot = rotate(keys.astype(jnp.float32).reshape(total_rows, kv_all, head_dim), offsets, rope_factors).astype(jnp.bfloat16)
    v_all = values.reshape(total_rows, kv_all, head_dim)
    k_pad = jnp.concatenate([jnp.zeros((pad_rows, kv_all, head_dim), jnp.bfloat16), k_rot], axis=0)
    v_pad = jnp.concatenate([jnp.zeros((pad_rows, kv_all, head_dim), jnp.bfloat16), v_all], axis=0)
    pos_pad = jnp.arange(total_rows + pad_rows, dtype=jnp.int32) - pad_rows
    doc_pad = jnp.concatenate([jnp.full((pad_rows,), -1, jnp.int32), doc_index])

    def per_block(block_number):
        first = (block_number * block_rows).astype(jnp.int32)
        q_block = lax.dynamic_slice_in_dim(q_rot, first, block_rows).reshape(block_rows, kv_all, group_size, head_dim)
        k_block = lax.dynamic_slice_in_dim(k_pad, first, span)
        v_block = lax.dynamic_slice_in_dim(v_pad, first, span)
        pos_k = lax.dynamic_slice_in_dim(pos_pad, first, span)
        doc_k = lax.dynamic_slice_in_dim(doc_pad, first, span)
        pos_q = first + jnp.arange(block_rows, dtype=jnp.int32)
        doc_q = lax.dynamic_slice_in_dim(doc_index, first, block_rows)
        visible = (doc_q[:, None] == doc_k[None, :]) & (pos_k[None, :] <= pos_q[:, None]) & (pos_k[None, :] >= 0)
        scores = jnp.einsum('qkgd,jkd->kgqj', q_block.astype(jnp.float32), k_block.astype(jnp.float32)) * score_scale
        scores = jnp.where(visible[None, None], scores, -1e+30)
        row_peak = lax.optimization_barrier(jnp.max(scores, axis=-1, keepdims=True))
        weights = jnp.exp(scores - row_peak)
        row_total = lax.optimization_barrier(jnp.sum(weights, axis=-1, keepdims=True))
        mixture = jnp.einsum('kgqj,jkd->qkgd', weights.astype(jnp.bfloat16).astype(jnp.float32), v_block.astype(jnp.float32))
        result = (mixture / row_total.transpose(2, 0, 1, 3)).astype(jnp.bfloat16)
        return result.reshape(block_rows, heads_all * head_dim)
    gathered = lax.map(per_block, jnp.arange(total_rows // block_rows, dtype=jnp.int32))
    gathered = gathered.reshape(total_rows, heads_all * head_dim)
    sources = source_table(owner_map)

    def owner_slots(sources_row):
        return slot_rows(sources_row, per_dev, block_rows)
    slot_table = jax.vmap(owner_slots)(sources)
    return gathered[slot_table.reshape(-1)]
```

```python
import functools
import math

import jax
import jax.numpy as jnp
from jax import lax
from jax.experimental import pallas as pl
from jax.experimental.pallas import tpu as pltpu
from jax.sharding import PartitionSpec as P

THETA = 500000.0


def passed_along(shard, axis, by):
    length = lax.axis_size(axis)
    pairs = [(i, i + by) for i in range(length) if 0 <= i + by < length]
    return lax.ppermute(shard, axis, pairs)


def doc_tables(lengths, positions):
    doc_ends = jnp.cumsum(lengths, dtype=jnp.int32)
    before = positions[:, None] >= doc_ends[None, :]
    doc_index = jnp.sum(before.astype(jnp.int32), axis=1, dtype=jnp.int32)
    doc_start = jnp.sum(jnp.where(before, lengths[None, :], 0), axis=1, dtype=jnp.int32)
    return (doc_index, positions - doc_start)


def inverse_freqs(factors, head_dim):
    half_dim = head_dim // 2
    exponent = jnp.arange(half_dim, dtype=jnp.float32) * (2.0 / head_dim)
    return 1.0 / (factors * jnp.power(jnp.float32(THETA), exponent))


def rotation_tables(offsets, inverse):
    angles = offsets.astype(jnp.float32)[:, None] * inverse[None, :]
    cosine = jnp.cos(angles)
    sine = jnp.sin(angles)
    return (
        jnp.concatenate([cosine, cosine], axis=1),
        jnp.concatenate([-sine, sine], axis=1),
    )


def rotate(vectors, offsets, inverse):
    half_dim = vectors.shape[-1] // 2
    angles = offsets.astype(jnp.float32)[:, None] * inverse[None, :]
    cosine = jnp.cos(angles)
    sine_part = jnp.sin(angles)
    first_half = vectors[..., :half_dim]
    second_half = vectors[..., half_dim:]
    return jnp.concatenate(
        [
            first_half * cosine - second_half * sine_part,
            second_half * cosine + first_half * sine_part,
        ],
        axis=-1,
    )


def attend_kernel(
    slot_ref, has_ref, q_ref, cos_ref, sin_ref, k_ref, v_ref, dq_ref, dk_ref, o_ref,
    *, heads, head_dim, block_rows, span, scale,
):
    d = pl.program_id(0)

    @pl.when(has_ref[d] == 0)
    def _():
        o_ref[...] = jnp.zeros_like(o_ref)

    @pl.when(has_ref[d] != 0)
    def _():
        start = pl.multiple_of(slot_ref[d] * block_rows, block_rows)
        k = k_ref[pl.ds(start, span), :]
        v = v_ref[pl.ds(start, span), :]
        doc_q = dq_ref[0]
        doc_k = dk_ref[0]
        tail = span - block_rows
        row = lax.broadcasted_iota(jnp.int32, (block_rows, span), 0)
        col = lax.broadcasted_iota(jnp.int32, (block_rows, span), 1)
        visible = (doc_q == doc_k) & (col <= row + tail)
        cos = cos_ref[...]
        sin = sin_ref[...]
        for h in range(heads):
            cols = slice(h * head_dim, (h + 1) * head_dim)
            qh = q_ref[:, cols].astype(jnp.float32)
            qr = (qh * cos + pltpu.roll(qh, head_dim // 2, 1) * sin).astype(jnp.bfloat16)
            s = lax.dot_general(
                qr, k, (((1,), (1,)), ((), ())), preferred_element_type=jnp.float32
            ) * scale
            s = jnp.where(visible, s, -1e30)
            m = jnp.max(s, axis=1, keepdims=True)
            p = jnp.exp(s - m)
            l = jnp.sum(p, axis=1, keepdims=True)
            o = jnp.dot(p.astype(jnp.bfloat16), v, preferred_element_type=jnp.float32)
            o_ref[0, :, cols] = (o / l).astype(o_ref.dtype)


def attend(slot, has, q, cos_t, sin_t, k_ext, v_ext, doc_q, doc_k, n_dest, head_dim):
    rows, width = q.shape
    per_dev, block_rows, _ = doc_q.shape
    span = doc_k.shape[2]
    ext_rows = k_ext.shape[0]
    heads = width // head_dim
    kernel = functools.partial(
        attend_kernel,
        heads=heads,
        head_dim=head_dim,
        block_rows=block_rows,
        span=span,
        scale=1.0 / math.sqrt(head_dim),
    )
    flops = 4 * per_dev * heads * block_rows * span * head_dim
    grid_spec = pltpu.PrefetchScalarGridSpec(
        num_scalar_prefetch=2,
        grid=(n_dest,),
        in_specs=[
            pl.BlockSpec((block_rows, width), lambda d, s, h: (s[d], 0)),
            pl.BlockSpec((block_rows, head_dim), lambda d, s, h: (s[d], 0)),
            pl.BlockSpec((block_rows, head_dim), lambda d, s, h: (s[d], 0)),
            pl.BlockSpec((ext_rows, head_dim), lambda d, s, h: (0, 0)),
            pl.BlockSpec((ext_rows, head_dim), lambda d, s, h: (0, 0)),
            pl.BlockSpec((1, block_rows, 1), lambda d, s, h: (s[d], 0, 0)),
            pl.BlockSpec((1, 1, span), lambda d, s, h: (s[d], 0, 0)),
        ],
        out_specs=pl.BlockSpec((1, block_rows, width), lambda d, s, h: (d, 0, 0)),
    )
    return pl.pallas_call(
        kernel,
        grid_spec=grid_spec,
        out_shape=jax.ShapeDtypeStruct((n_dest, block_rows, width), q.dtype),
        cost_estimate=pl.CostEstimate(
            flops=flops,
            transcendentals=per_dev * heads * block_rows * span,
            bytes_accessed=2 * rows * width * 2 + 2 * ext_rows * head_dim * 2,
        ),
    )(slot, has, q, cos_t, sin_t, k_ext, v_ext, doc_q, doc_k)


def local(queries, keys, values, rope_factors, doc_lengths, owner_map):
    ctx_size = lax.axis_size("ctx")
    ctx_index = lax.axis_index("ctx")
    tp_size = lax.axis_size("tp")
    row_count = queries.shape[0]
    per_dev = owner_map.shape[1]
    block_rows = row_count // per_dev
    tail_rows = row_count // 4
    span = tail_rows + block_rows
    head_dim = 2 * rope_factors.shape[0]
    kv_heads = keys.shape[1] // head_dim
    kv_local = kv_heads // tp_size
    shard_rows = keys.shape[0]

    kv = jnp.stack(
        [
            keys.reshape(shard_rows, tp_size, kv_local * head_dim),
            values.reshape(shard_rows, tp_size, kv_local * head_dim),
        ],
        axis=2,
    ).reshape(shard_rows, tp_size * 2 * kv_local * head_dim)
    kv = lax.all_to_all(kv, "tp", split_axis=1, concat_axis=0, tiled=True)
    kv_tail = passed_along(kv[row_count - tail_rows :], "ctx", 1)
    kv_ext = jnp.concatenate([kv_tail, kv], axis=0)
    kv_width = kv_local * head_dim
    k_raw = kv_ext[:, :kv_width]
    v_ext = kv_ext[:, kv_width:]

    ext_rows = row_count + tail_rows
    pos_ext = ctx_index * row_count - tail_rows + jnp.arange(ext_rows, dtype=jnp.int32)
    doc_ext, off_ext = doc_tables(doc_lengths, pos_ext)
    doc_ext = jnp.where(pos_ext >= 0, doc_ext, -1)
    inverse = inverse_freqs(rope_factors, head_dim)
    k_ext = rotate(k_raw.astype(jnp.float32), off_ext, inverse).astype(jnp.bfloat16)
    cos_t, sin_t = rotation_tables(off_ext[tail_rows:], inverse)

    doc_q = doc_ext[tail_rows:].reshape(per_dev, block_rows, 1)
    doc_k = jnp.stack(
        [doc_ext[slot * block_rows : slot * block_rows + span] for slot in range(per_dev)]
    ).reshape(per_dev, 1, span)

    devices = jnp.arange(ctx_size, dtype=jnp.int32)
    owner_row = lax.dynamic_index_in_dim(owner_map, ctx_index, 0, keepdims=False)
    match = owner_row[None, :] == devices[:, None]
    has = jnp.sum(match.astype(jnp.int32), axis=1, dtype=jnp.int32)
    slot = jnp.sum(
        jnp.where(match, jnp.arange(per_dev, dtype=jnp.int32)[None, :], 0), axis=1, dtype=jnp.int32
    )

    send = attend(
        slot, has, queries, cos_t, sin_t, k_ext, v_ext, doc_q, doc_k, ctx_size, head_dim
    )
    arrived = lax.all_to_all(send, "ctx", split_axis=0, concat_axis=0, tiled=True)

    sources_match = owner_map == ctx_index
    my_sources = jnp.sum(
        jnp.where(sources_match, devices[:, None], 0), axis=0, dtype=jnp.int32
    )
    finished = jnp.take(arrived, my_sources, axis=0)
    return finished.reshape(row_count, queries.shape[1])


def solution(mesh):
    in_specs = (P("ctx", "tp"), P(("ctx", "tp"), None), P(("ctx", "tp"), None), P(), P(), P())
    out_specs = P("ctx", "tp")
    return jax.shard_map(local, mesh=mesh, in_specs=in_specs, out_specs=out_specs, check_vma=False)
```

```python
import functools
import math

import jax
import jax.numpy as jnp
from jax import lax
from jax.experimental import pallas as pl
from jax.experimental.pallas import tpu as pltpu
from jax.sharding import PartitionSpec as P

THETA = 500000.0


def passed_along(shard, axis, by):
    length = lax.axis_size(axis)
    pairs = [(i, i + by) for i in range(length) if 0 <= i + by < length]
    return lax.ppermute(shard, axis, pairs)


def doc_tables(lengths, positions):
    doc_ends = jnp.cumsum(lengths, dtype=jnp.int32)
    before = positions[:, None] >= doc_ends[None, :]
    doc_index = jnp.sum(before.astype(jnp.int32), axis=1, dtype=jnp.int32)
    doc_start = jnp.sum(jnp.where(before, lengths[None, :], 0), axis=1, dtype=jnp.int32)
    return (doc_index, positions - doc_start)


def inverse_freqs(factors, head_dim):
    half_dim = head_dim // 2
    exponent = jnp.arange(half_dim, dtype=jnp.float32) * (2.0 / head_dim)
    return 1.0 / (factors * jnp.power(jnp.float32(THETA), exponent))


def rotation_tables(offsets, inverse):
    angles = offsets.astype(jnp.float32)[:, None] * inverse[None, :]
    cosine = jnp.cos(angles)
    sine = jnp.sin(angles)
    return (
        jnp.concatenate([cosine, cosine], axis=1),
        jnp.concatenate([-sine, sine], axis=1),
    )


def rotate(vectors, offsets, inverse):
    half_dim = vectors.shape[-1] // 2
    angles = offsets.astype(jnp.float32)[:, None] * inverse[None, :]
    cosine = jnp.cos(angles)
    sine_part = jnp.sin(angles)
    first_half = vectors[..., :half_dim]
    second_half = vectors[..., half_dim:]
    return jnp.concatenate(
        [
            first_half * cosine - second_half * sine_part,
            second_half * cosine + first_half * sine_part,
        ],
        axis=-1,
    )


def attend_kernel(
    slot_ref, has_ref, q_ref, cos_ref, sin_ref, k_ref, v_ref, dq_ref, dk_ref, o_ref,
    *, heads, head_dim, block_rows, span, scale,
):
    d = pl.program_id(0)

    @pl.when(has_ref[d] == 0)
    def _():
        o_ref[...] = jnp.zeros_like(o_ref)

    @pl.when(has_ref[d] != 0)
    def _():
        start = pl.multiple_of(slot_ref[d] * block_rows, block_rows)
        k = k_ref[pl.ds(start, span), :]
        v = v_ref[pl.ds(start, span), :]
        doc_q = dq_ref[0]
        doc_k = dk_ref[0]
        tail = span - block_rows
        row = lax.broadcasted_iota(jnp.int32, (block_rows, span), 0)
        col = lax.broadcasted_iota(jnp.int32, (block_rows, span), 1)
        visible = (doc_q == doc_k) & (col <= row + tail)
        cos = cos_ref[...]
        sin = sin_ref[...]
        for h in range(heads):
            cols = slice(h * head_dim, (h + 1) * head_dim)
            qh = q_ref[:, cols].astype(jnp.float32)
            qr = (qh * cos + pltpu.roll(qh, head_dim // 2, 1) * sin).astype(jnp.bfloat16)
            s = lax.dot_general(
                qr, k, (((1,), (1,)), ((), ())), preferred_element_type=jnp.float32
            ) * scale
            s = jnp.where(visible, s, -1e30)
            m = jnp.max(s, axis=1, keepdims=True)
            p = jnp.exp(s - m)
            l = jnp.sum(p, axis=1, keepdims=True)
            o = jnp.dot(p.astype(jnp.bfloat16), v, preferred_element_type=jnp.float32)
            o_ref[0, :, cols] = (o / l).astype(o_ref.dtype)


def attend(slot, has, q, cos_t, sin_t, k_ext, v_ext, doc_q, doc_k, n_dest, head_dim):
    rows, width = q.shape
    per_dev, block_rows, _ = doc_q.shape
    span = doc_k.shape[2]
    ext_rows = k_ext.shape[0]
    heads = width // head_dim
    kernel = functools.partial(
        attend_kernel,
        heads=heads,
        head_dim=head_dim,
        block_rows=block_rows,
        span=span,
        scale=1.0 / math.sqrt(head_dim),
    )
    flops = 4 * per_dev * heads * block_rows * span * head_dim
    grid_spec = pltpu.PrefetchScalarGridSpec(
        num_scalar_prefetch=2,
        grid=(n_dest,),
        in_specs=[
            pl.BlockSpec((block_rows, width), lambda d, s, h: (s[d], 0)),
            pl.BlockSpec((block_rows, head_dim), lambda d, s, h: (s[d], 0)),
            pl.BlockSpec((block_rows, head_dim), lambda d, s, h: (s[d], 0)),
            pl.BlockSpec((ext_rows, head_dim), lambda d, s, h: (0, 0)),
            pl.BlockSpec((ext_rows, head_dim), lambda d, s, h: (0, 0)),
            pl.BlockSpec((1, block_rows, 1), lambda d, s, h: (s[d], 0, 0)),
            pl.BlockSpec((1, 1, span), lambda d, s, h: (s[d], 0, 0)),
        ],
        out_specs=pl.BlockSpec((1, block_rows, width), lambda d, s, h: (d, 0, 0)),
    )
    return pl.pallas_call(
        kernel,
        grid_spec=grid_spec,
        out_shape=jax.ShapeDtypeStruct((n_dest, block_rows, width), q.dtype),
        cost_estimate=pl.CostEstimate(
            flops=flops,
            transcendentals=per_dev * heads * block_rows * span,
            bytes_accessed=2 * rows * width * 2 + 2 * ext_rows * head_dim * 2,
        ),
    )(slot, has, q, cos_t, sin_t, k_ext, v_ext, doc_q, doc_k)


def local(queries, keys, values, rope_factors, doc_lengths, owner_map):
    ctx_size = lax.axis_size("ctx")
    ctx_index = lax.axis_index("ctx")
    tp_size = lax.axis_size("tp")
    row_count = queries.shape[0]
    per_dev = owner_map.shape[1]
    block_rows = row_count // per_dev
    tail_rows = row_count // 4
    span = tail_rows + block_rows
    head_dim = 2 * rope_factors.shape[0]
    kv_heads = keys.shape[1] // head_dim
    kv_local = kv_heads // tp_size
    shard_rows = keys.shape[0]

    kv = jnp.stack(
        [
            keys.reshape(shard_rows, tp_size, kv_local * head_dim),
            values.reshape(shard_rows, tp_size, kv_local * head_dim),
        ],
        axis=2,
    ).reshape(shard_rows, tp_size * 2 * kv_local * head_dim)
    kv = lax.all_to_all(kv, "tp", split_axis=1, concat_axis=0, tiled=True)
    kv_tail = passed_along(kv[row_count - tail_rows :], "ctx", 1)
    kv_ext = jnp.concatenate([kv_tail, kv], axis=0)
    kv_width = kv_local * head_dim
    k_raw = kv_ext[:, :kv_width]
    v_ext = kv_ext[:, kv_width:]

    ext_rows = row_count + tail_rows
    pos_ext = ctx_index * row_count - tail_rows + jnp.arange(ext_rows, dtype=jnp.int32)
    doc_ext, off_ext = doc_tables(doc_lengths, pos_ext)
    doc_ext = jnp.where(pos_ext >= 0, doc_ext, -1)
    inverse = inverse_freqs(rope_factors, head_dim)
    k_ext = rotate(k_raw.astype(jnp.float32), off_ext, inverse).astype(jnp.bfloat16)
    cos_t, sin_t = rotation_tables(off_ext[tail_rows:], inverse)

    doc_q = doc_ext[tail_rows:].reshape(per_dev, block_rows, 1)
    doc_k = jnp.stack(
        [doc_ext[slot * block_rows : slot * block_rows + span] for slot in range(per_dev)]
    ).reshape(per_dev, 1, span)

    devices = jnp.arange(ctx_size, dtype=jnp.int32)
    owner_row = lax.dynamic_index_in_dim(owner_map, ctx_index, 0, keepdims=False)
    dest = lax.rem(ctx_index + devices, ctx_size)
    match = owner_row[None, :] == dest[:, None]
    has = jnp.sum(match.astype(jnp.int32), axis=1, dtype=jnp.int32)
    slot = jnp.sum(
        jnp.where(match, jnp.arange(per_dev, dtype=jnp.int32)[None, :], 0), axis=1, dtype=jnp.int32
    )

    send = attend(
        slot, has, queries, cos_t, sin_t, k_ext, v_ext, doc_q, doc_k, ctx_size, head_dim
    )
    pieces = [send[0]]
    for shift in range(1, ctx_size):
        pairs = [(i, (i + shift) % ctx_size) for i in range(ctx_size)]
        pieces.append(lax.ppermute(send[shift], "ctx", pairs))
    arrived = jnp.stack(pieces)

    sources_match = owner_map == ctx_index
    my_sources = jnp.sum(
        jnp.where(sources_match, devices[:, None], 0), axis=0, dtype=jnp.int32
    )
    shifts = lax.rem(ctx_index - my_sources + ctx_size, ctx_size)
    finished = jnp.take(arrived, shifts, axis=0)
    return finished.reshape(row_count, queries.shape[1])


def solution(mesh):
    in_specs = (P("ctx", "tp"), P(("ctx", "tp"), None), P(("ctx", "tp"), None), P(), P(), P())
    out_specs = P("ctx", "tp")
    return jax.shard_map(local, mesh=mesh, in_specs=in_specs, out_specs=out_specs, check_vma=False)
```

```python
import functools
import math

import jax
import jax.numpy as jnp
from jax import lax
from jax.experimental import pallas as pl
from jax.experimental.pallas import tpu as pltpu
from jax.sharding import PartitionSpec as P

THETA = 500000.0


def passed_along(shard, axis, by):
    length = lax.axis_size(axis)
    pairs = [(i, i + by) for i in range(length) if 0 <= i + by < length]
    return lax.ppermute(shard, axis, pairs)


def doc_tables(lengths, positions):
    doc_ends = jnp.cumsum(lengths, dtype=jnp.int32)
    before = positions[:, None] >= doc_ends[None, :]
    doc_index = jnp.sum(before.astype(jnp.int32), axis=1, dtype=jnp.int32)
    doc_start = jnp.sum(jnp.where(before, lengths[None, :], 0), axis=1, dtype=jnp.int32)
    return (doc_index, positions - doc_start)


def inverse_freqs(factors, head_dim):
    half_dim = head_dim // 2
    exponent = jnp.arange(half_dim, dtype=jnp.float32) * (2.0 / head_dim)
    return 1.0 / (factors * jnp.power(jnp.float32(THETA), exponent))


def rotation_tables(offsets, inverse):
    angles = offsets.astype(jnp.float32)[:, None] * inverse[None, :]
    cosine = jnp.cos(angles)
    sine = jnp.sin(angles)
    return (
        jnp.concatenate([cosine, cosine], axis=1),
        jnp.concatenate([-sine, sine], axis=1),
    )


def rotate(vectors, offsets, inverse):
    half_dim = vectors.shape[-1] // 2
    angles = offsets.astype(jnp.float32)[:, None] * inverse[None, :]
    cosine = jnp.cos(angles)
    sine_part = jnp.sin(angles)
    first_half = vectors[..., :half_dim]
    second_half = vectors[..., half_dim:]
    return jnp.concatenate(
        [
            first_half * cosine - second_half * sine_part,
            second_half * cosine + first_half * sine_part,
        ],
        axis=-1,
    )


def attend_kernel(
    slot_ref, has_ref, q_ref, cos_ref, sin_ref, k_ref, v_ref, dq_ref, dk_ref, o_ref,
    *, heads, head_dim, block_rows, span, scale,
):
    d = pl.program_id(0)

    @pl.when(has_ref[d] == 0)
    def _():
        o_ref[...] = jnp.zeros_like(o_ref)

    @pl.when(has_ref[d] != 0)
    def _():
        start = pl.multiple_of(slot_ref[d] * block_rows, block_rows)
        k = k_ref[pl.ds(start, span), :]
        v = v_ref[pl.ds(start, span), :]
        doc_q = dq_ref[0]
        doc_k = dk_ref[0]
        tail = span - block_rows
        row = lax.broadcasted_iota(jnp.int32, (block_rows, span), 0)
        col = lax.broadcasted_iota(jnp.int32, (block_rows, span), 1)
        visible = (doc_q == doc_k) & (col <= row + tail)
        cos = cos_ref[...]
        sin = sin_ref[...]
        for h in range(heads):
            cols = slice(h * head_dim, (h + 1) * head_dim)
            qh = q_ref[:, cols].astype(jnp.float32)
            qr = (qh * cos + pltpu.roll(qh, head_dim // 2, 1) * sin).astype(jnp.bfloat16)
            s = lax.dot_general(
                qr, k, (((1,), (1,)), ((), ())), preferred_element_type=jnp.float32
            ) * scale
            s = jnp.where(visible, s, -1e30)
            m = jnp.max(s, axis=1, keepdims=True)
            p = jnp.exp(s - m)
            l = jnp.sum(p, axis=1, keepdims=True)
            o = jnp.dot(p.astype(jnp.bfloat16), v, preferred_element_type=jnp.float32)
            o_ref[0, :, cols] = (o / l).astype(o_ref.dtype)


def attend(slot, has, q, cos_t, sin_t, k_ext, v_ext, doc_q, doc_k, n_dest, head_dim, group, groups):
    rows, all_width = q.shape
    width = all_width // groups
    per_dev, block_rows, _ = doc_q.shape
    span = doc_k.shape[2]
    ext_rows = k_ext.shape[0]
    heads = width // head_dim
    kernel = functools.partial(
        attend_kernel,
        heads=heads,
        head_dim=head_dim,
        block_rows=block_rows,
        span=span,
        scale=1.0 / math.sqrt(head_dim),
    )
    flops = 4 * per_dev * heads * block_rows * span * head_dim
    grid_spec = pltpu.PrefetchScalarGridSpec(
        num_scalar_prefetch=2,
        grid=(n_dest,),
        in_specs=[
            pl.BlockSpec((block_rows, width), lambda d, s, h: (s[d], group)),
            pl.BlockSpec((block_rows, head_dim), lambda d, s, h: (s[d], 0)),
            pl.BlockSpec((block_rows, head_dim), lambda d, s, h: (s[d], 0)),
            pl.BlockSpec((ext_rows, head_dim), lambda d, s, h: (0, 0)),
            pl.BlockSpec((ext_rows, head_dim), lambda d, s, h: (0, 0)),
            pl.BlockSpec((1, block_rows, 1), lambda d, s, h: (s[d], 0, 0)),
            pl.BlockSpec((1, 1, span), lambda d, s, h: (s[d], 0, 0)),
        ],
        out_specs=pl.BlockSpec((1, block_rows, width), lambda d, s, h: (d, 0, 0)),
    )
    return pl.pallas_call(
        kernel,
        grid_spec=grid_spec,
        out_shape=jax.ShapeDtypeStruct((n_dest, block_rows, width), q.dtype),
        cost_estimate=pl.CostEstimate(
            flops=flops,
            transcendentals=per_dev * heads * block_rows * span,
            bytes_accessed=rows * width * 2 + n_dest * block_rows * width * 2
            + 2 * ext_rows * head_dim * 2,
        ),
    )(slot, has, q, cos_t, sin_t, k_ext, v_ext, doc_q, doc_k)


def local(queries, keys, values, rope_factors, doc_lengths, owner_map):
    ctx_size = lax.axis_size("ctx")
    ctx_index = lax.axis_index("ctx")
    tp_size = lax.axis_size("tp")
    row_count = queries.shape[0]
    per_dev = owner_map.shape[1]
    block_rows = row_count // per_dev
    tail_rows = row_count // 4
    span = tail_rows + block_rows
    head_dim = 2 * rope_factors.shape[0]
    kv_heads = keys.shape[1] // head_dim
    kv_local = kv_heads // tp_size
    shard_rows = keys.shape[0]

    kv = jnp.stack(
        [
            keys.reshape(shard_rows, tp_size, kv_local * head_dim),
            values.reshape(shard_rows, tp_size, kv_local * head_dim),
        ],
        axis=2,
    ).reshape(shard_rows, tp_size * 2 * kv_local * head_dim)
    kv = lax.all_to_all(kv, "tp", split_axis=1, concat_axis=0, tiled=True)
    kv_tail = passed_along(kv[row_count - tail_rows :], "ctx", 1)
    kv_ext = jnp.concatenate([kv_tail, kv], axis=0)
    kv_width = kv_local * head_dim
    k_raw = kv_ext[:, :kv_width]
    v_ext = kv_ext[:, kv_width:]

    ext_rows = row_count + tail_rows
    pos_ext = ctx_index * row_count - tail_rows + jnp.arange(ext_rows, dtype=jnp.int32)
    doc_ext, off_ext = doc_tables(doc_lengths, pos_ext)
    doc_ext = jnp.where(pos_ext >= 0, doc_ext, -1)
    inverse = inverse_freqs(rope_factors, head_dim)
    cos_ext, sin_ext = rotation_tables(off_ext, inverse)
    k_f = k_raw.astype(jnp.float32)
    k_ext = (k_f * cos_ext + jnp.roll(k_f, head_dim // 2, axis=1) * sin_ext).astype(jnp.bfloat16)
    cos_t = cos_ext[tail_rows:]
    sin_t = sin_ext[tail_rows:]

    doc_q = doc_ext[tail_rows:].reshape(per_dev, block_rows, 1)
    doc_k = jnp.stack(
        [doc_ext[slot * block_rows : slot * block_rows + span] for slot in range(per_dev)]
    ).reshape(per_dev, 1, span)

    devices = jnp.arange(ctx_size, dtype=jnp.int32)
    owner_row = lax.dynamic_index_in_dim(owner_map, ctx_index, 0, keepdims=False)
    match = owner_row[None, :] == devices[:, None]
    has = jnp.sum(match.astype(jnp.int32), axis=1, dtype=jnp.int32)
    slot = jnp.sum(
        jnp.where(match, jnp.arange(per_dev, dtype=jnp.int32)[None, :], 0), axis=1, dtype=jnp.int32
    )

    groups = 4
    arrived = []
    for group in range(groups):
        send = attend(
            slot, has, queries, cos_t, sin_t, k_ext, v_ext, doc_q, doc_k, ctx_size, head_dim,
            group, groups,
        )
        arrived.append(lax.all_to_all(send, "ctx", split_axis=0, concat_axis=0, tiled=True))

    sources_match = owner_map == ctx_index
    my_sources = jnp.sum(
        jnp.where(sources_match, devices[:, None], 0), axis=0, dtype=jnp.int32
    )
    finished = jnp.concatenate([jnp.take(a, my_sources, axis=0) for a in arrived], axis=-1)
    return finished.reshape(row_count, queries.shape[1])


def solution(mesh):
    in_specs = (P("ctx", "tp"), P(("ctx", "tp"), None), P(("ctx", "tp"), None), P(), P(), P())
    out_specs = P("ctx", "tp")
    return jax.shard_map(local, mesh=mesh, in_specs=in_specs, out_specs=out_specs, check_vma=False)
```

```python
import functools
import math

import jax
import jax.numpy as jnp
from jax import lax
from jax.experimental import pallas as pl
from jax.experimental.pallas import tpu as pltpu
from jax.sharding import PartitionSpec as P

THETA = 500000.0


def passed_along(shard, axis, by):
    length = lax.axis_size(axis)
    pairs = [(i, i + by) for i in range(length) if 0 <= i + by < length]
    return lax.ppermute(shard, axis, pairs)


def doc_tables(lengths, positions):
    doc_ends = jnp.cumsum(lengths, dtype=jnp.int32)
    before = positions[:, None] >= doc_ends[None, :]
    doc_index = jnp.sum(before.astype(jnp.int32), axis=1, dtype=jnp.int32)
    doc_start = jnp.sum(jnp.where(before, lengths[None, :], 0), axis=1, dtype=jnp.int32)
    return (doc_index, positions - doc_start)


def inverse_freqs(factors, head_dim):
    half_dim = head_dim // 2
    exponent = jnp.arange(half_dim, dtype=jnp.float32) * (2.0 / head_dim)
    return 1.0 / (factors * jnp.power(jnp.float32(THETA), exponent))


def rotation_tables(offsets, inverse, distinct):
    angles = jnp.arange(distinct, dtype=jnp.int32).astype(jnp.float32)[:, None] * inverse[None, :]
    cosine = jnp.cos(angles)
    sine = jnp.sin(angles)
    table = jnp.concatenate([cosine, cosine, -sine, sine], axis=1)
    rows = jnp.take(table, jnp.clip(offsets, 0, distinct - 1), axis=0, mode="clip")
    half = 2 * inverse.shape[0]
    return rows[:, :half], rows[:, half:]


def rotate(vectors, offsets, inverse):
    half_dim = vectors.shape[-1] // 2
    angles = offsets.astype(jnp.float32)[:, None] * inverse[None, :]
    cosine = jnp.cos(angles)
    sine_part = jnp.sin(angles)
    first_half = vectors[..., :half_dim]
    second_half = vectors[..., half_dim:]
    return jnp.concatenate(
        [
            first_half * cosine - second_half * sine_part,
            second_half * cosine + first_half * sine_part,
        ],
        axis=-1,
    )


def attend_kernel(slot_ref, has_ref, *refs, heads, head_dim, block_rows, span, scale):
    q_refs = refs[:heads]
    cos_ref, sin_ref, k_ref, v_ref, dq_ref, dk_ref, o_ref = refs[heads:]
    d = pl.program_id(0)

    @pl.when(has_ref[d] == 0)
    def _():
        o_ref[...] = jnp.zeros_like(o_ref)

    @pl.when(has_ref[d] != 0)
    def _():
        start = pl.multiple_of(slot_ref[d] * block_rows, block_rows)
        k = k_ref[pl.ds(start, span), :]
        v = v_ref[pl.ds(start, span), :]
        doc_q = dq_ref[0]
        doc_k = dk_ref[0]
        tail = span - block_rows
        row = lax.broadcasted_iota(jnp.int32, (block_rows, span), 0)
        col = lax.broadcasted_iota(jnp.int32, (block_rows, span), 1)
        visible = (doc_q == doc_k) & (col <= row + tail)
        cos = cos_ref[...]
        sin = sin_ref[...]
        for h in range(heads):
            cols = slice(h * head_dim, (h + 1) * head_dim)
            qh = q_refs[h][...].astype(jnp.float32)
            qr = (qh * cos + pltpu.roll(qh, head_dim // 2, 1) * sin).astype(jnp.bfloat16)
            s = lax.dot_general(
                qr, k, (((1,), (1,)), ((), ())), preferred_element_type=jnp.float32
            ) * scale
            s = jnp.where(visible, s, -1e30)
            m = jnp.max(s, axis=1, keepdims=True)
            p = jnp.exp(s - m)
            l = jnp.sum(p, axis=1, keepdims=True)
            o = jnp.dot(p.astype(jnp.bfloat16), v, preferred_element_type=jnp.float32)
            o_ref[0, :, cols] = (o / l).astype(o_ref.dtype)


def attend(slot, has, q, cos_t, sin_t, k_ext, v_ext, doc_q, doc_k, n_dest, head_dim, first, heads):
    rows, all_width = q.shape
    width = heads * head_dim
    per_dev, block_rows, _ = doc_q.shape
    span = doc_k.shape[2]
    ext_rows = k_ext.shape[0]
    kernel = functools.partial(
        attend_kernel,
        heads=heads,
        head_dim=head_dim,
        block_rows=block_rows,
        span=span,
        scale=1.0 / math.sqrt(head_dim),
    )
    flops = 4 * per_dev * heads * block_rows * span * head_dim
    grid_spec = pltpu.PrefetchScalarGridSpec(
        num_scalar_prefetch=2,
        grid=(n_dest,),
        in_specs=[
            pl.BlockSpec((block_rows, head_dim), functools.partial(
                lambda d, s, h, col: (s[d], col), col=first + head))
            for head in range(heads)
        ] + [
            pl.BlockSpec((block_rows, head_dim), lambda d, s, h: (s[d], 0)),
            pl.BlockSpec((block_rows, head_dim), lambda d, s, h: (s[d], 0)),
            pl.BlockSpec((ext_rows, head_dim), lambda d, s, h: (0, 0)),
            pl.BlockSpec((ext_rows, head_dim), lambda d, s, h: (0, 0)),
            pl.BlockSpec((1, block_rows, 1), lambda d, s, h: (s[d], 0, 0)),
            pl.BlockSpec((1, 1, span), lambda d, s, h: (s[d], 0, 0)),
        ],
        out_specs=pl.BlockSpec((1, block_rows, width), lambda d, s, h: (d, 0, 0)),
    )
    return pl.pallas_call(
        kernel,
        grid_spec=grid_spec,
        out_shape=jax.ShapeDtypeStruct((n_dest, block_rows, width), q.dtype),
        cost_estimate=pl.CostEstimate(
            flops=flops,
            transcendentals=per_dev * heads * block_rows * span,
            bytes_accessed=rows * width * 2 + n_dest * block_rows * width * 2
            + 2 * ext_rows * head_dim * 2,
        ),
    )(slot, has, *([q] * heads), cos_t, sin_t, k_ext, v_ext, doc_q, doc_k)


def local(queries, keys, values, rope_factors, doc_lengths, owner_map):
    ctx_size = lax.axis_size("ctx")
    ctx_index = lax.axis_index("ctx")
    tp_size = lax.axis_size("tp")
    row_count = queries.shape[0]
    per_dev = owner_map.shape[1]
    block_rows = row_count // per_dev
    tail_rows = row_count // 4
    span = tail_rows + block_rows
    head_dim = 2 * rope_factors.shape[0]
    kv_heads = keys.shape[1] // head_dim
    kv_local = kv_heads // tp_size
    shard_rows = keys.shape[0]

    kv = jnp.stack(
        [
            keys.reshape(shard_rows, tp_size, kv_local * head_dim),
            values.reshape(shard_rows, tp_size, kv_local * head_dim),
        ],
        axis=2,
    ).reshape(shard_rows, tp_size * 2 * kv_local * head_dim)
    kv = lax.all_to_all(kv, "tp", split_axis=1, concat_axis=0, tiled=True)
    kv_tail = passed_along(kv[row_count - tail_rows :], "ctx", 1)
    kv_ext = jnp.concatenate([kv_tail, kv], axis=0)
    kv_width = kv_local * head_dim
    k_raw = kv_ext[:, :kv_width]
    v_ext = kv_ext[:, kv_width:]

    ext_rows = row_count + tail_rows
    pos_ext = ctx_index * row_count - tail_rows + jnp.arange(ext_rows, dtype=jnp.int32)
    doc_ext, off_ext = doc_tables(doc_lengths, pos_ext)
    doc_ext = jnp.where(pos_ext >= 0, doc_ext, -1)
    inverse = inverse_freqs(rope_factors, head_dim)
    cos_ext, sin_ext = rotation_tables(off_ext, inverse, tail_rows)
    k_f = k_raw.astype(jnp.float32)
    k_ext = (k_f * cos_ext + jnp.roll(k_f, head_dim // 2, axis=1) * sin_ext).astype(jnp.bfloat16)
    cos_t = cos_ext[tail_rows:]
    sin_t = sin_ext[tail_rows:]

    doc_q = doc_ext[tail_rows:].reshape(per_dev, block_rows, 1)
    doc_k = jnp.stack(
        [doc_ext[slot * block_rows : slot * block_rows + span] for slot in range(per_dev)]
    ).reshape(per_dev, 1, span)

    devices = jnp.arange(ctx_size, dtype=jnp.int32)
    owner_row = lax.dynamic_index_in_dim(owner_map, ctx_index, 0, keepdims=False)
    match = owner_row[None, :] == devices[:, None]
    has = jnp.sum(match.astype(jnp.int32), axis=1, dtype=jnp.int32)
    slot = jnp.sum(
        jnp.where(match, jnp.arange(per_dev, dtype=jnp.int32)[None, :], 0), axis=1, dtype=jnp.int32
    )

    q_heads = queries.shape[1] // head_dim
    sizes = [1, 2, 2, 2, 1] if q_heads == 8 else [q_heads]
    arrived = []
    first = 0
    for heads in sizes:
        send = attend(
            slot, has, queries, cos_t, sin_t, k_ext, v_ext, doc_q, doc_k, ctx_size, head_dim,
            first, heads,
        )
        arrived.append(lax.all_to_all(send, "ctx", split_axis=0, concat_axis=0, tiled=True))
        first += heads

    sources_match = owner_map == ctx_index
    my_sources = jnp.sum(
        jnp.where(sources_match, devices[:, None], 0), axis=0, dtype=jnp.int32
    )
    finished = jnp.concatenate(
        [jnp.take(a, my_sources, axis=0, mode="clip") for a in arrived], axis=-1
    )
    return finished.reshape(row_count, queries.shape[1])


def solution(mesh):
    in_specs = (P("ctx", "tp"), P(("ctx", "tp"), None), P(("ctx", "tp"), None), P(), P(), P())
    out_specs = P("ctx", "tp")
    return jax.shard_map(local, mesh=mesh, in_specs=in_specs, out_specs=out_specs, check_vma=False)
```

```python
import functools
import math

import jax
import jax.numpy as jnp
from jax import lax
from jax.experimental import pallas as pl
from jax.experimental.pallas import tpu as pltpu
from jax.sharding import PartitionSpec as P

THETA = 500000.0


def passed_along(shard, axis, by):
    length = lax.axis_size(axis)
    pairs = [(i, i + by) for i in range(length) if 0 <= i + by < length]
    return lax.ppermute(shard, axis, pairs)


def doc_tables(lengths, positions):
    doc_ends = jnp.cumsum(lengths, dtype=jnp.int32)
    before = positions[:, None] >= doc_ends[None, :]
    doc_index = jnp.sum(before.astype(jnp.int32), axis=1, dtype=jnp.int32)
    doc_start = jnp.sum(jnp.where(before, lengths[None, :], 0), axis=1, dtype=jnp.int32)
    return (doc_index, positions - doc_start)


def inverse_freqs(factors, head_dim):
    half_dim = head_dim // 2
    exponent = jnp.arange(half_dim, dtype=jnp.float32) * (2.0 / head_dim)
    return 1.0 / (factors * jnp.power(jnp.float32(THETA), exponent))


def rotation_tables(offsets, inverse, distinct):
    angles = jnp.arange(distinct, dtype=jnp.int32).astype(jnp.float32)[:, None] * inverse[None, :]
    cosine = jnp.cos(angles)
    sine = jnp.sin(angles)
    table = jnp.concatenate([cosine, cosine, -sine, sine], axis=1)
    rows = jnp.take(table, jnp.clip(offsets, 0, distinct - 1), axis=0, mode="clip")
    half = 2 * inverse.shape[0]
    return rows[:, :half], rows[:, half:]


def rotate(vectors, offsets, inverse):
    half_dim = vectors.shape[-1] // 2
    angles = offsets.astype(jnp.float32)[:, None] * inverse[None, :]
    cosine = jnp.cos(angles)
    sine_part = jnp.sin(angles)
    first_half = vectors[..., :half_dim]
    second_half = vectors[..., half_dim:]
    return jnp.concatenate(
        [
            first_half * cosine - second_half * sine_part,
            second_half * cosine + first_half * sine_part,
        ],
        axis=-1,
    )


def attend_kernel(dest_ref, *refs, heads, head_dim, block_rows, span, scale):
    q_refs = refs[:heads]
    cos_ref, sin_ref, k_ref, v_ref, lo_ref, o_ref = refs[heads:]
    r = pl.program_id(0)
    if True:
        start = pl.multiple_of(r * block_rows, block_rows)
        k = k_ref[pl.ds(start, span), :]
        v = v_ref[pl.ds(start, span), :]
        tail = span - block_rows
        lo = lo_ref[0]
        hi = lax.broadcasted_iota(jnp.int32, (block_rows, 1), 0) + tail
        col = lax.broadcasted_iota(jnp.int32, (block_rows, span), 1)
        visible = (col >= lo) & (col <= hi)
        cos = cos_ref[...]
        sin = sin_ref[...]
        for h in range(heads):
            cols = slice(h * head_dim, (h + 1) * head_dim)
            qh = q_refs[h][...].astype(jnp.float32)
            qr = (qh * cos + pltpu.roll(qh, head_dim // 2, 1) * sin).astype(jnp.bfloat16)
            s = lax.dot_general(
                qr, k, (((1,), (1,)), ((), ())), preferred_element_type=jnp.float32
            ) * scale
            s = jnp.where(visible, s, -1e30)
            m = jnp.max(s, axis=1, keepdims=True)
            p = jnp.exp(s - m)
            l = jnp.sum(p, axis=1, keepdims=True)
            o = jnp.dot(p.astype(jnp.bfloat16), v, preferred_element_type=jnp.float32)
            o_ref[0, :, cols] = (o / l).astype(o_ref.dtype)


def attend(dest, q, cos_t, sin_t, k_ext, v_ext, lo, n_dest, head_dim, first, heads):
    rows, all_width = q.shape
    width = heads * head_dim
    per_dev, block_rows, _ = lo.shape
    ext_rows = k_ext.shape[0]
    span = ext_rows - rows + block_rows
    kernel = functools.partial(
        attend_kernel,
        heads=heads,
        head_dim=head_dim,
        block_rows=block_rows,
        span=span,
        scale=1.0 / math.sqrt(head_dim),
    )
    flops = 4 * per_dev * heads * block_rows * span * head_dim
    grid_spec = pltpu.PrefetchScalarGridSpec(
        num_scalar_prefetch=1,
        grid=(per_dev,),
        in_specs=[
            pl.BlockSpec((block_rows, head_dim), functools.partial(
                lambda r, dst, col: (r, col), col=first + head))
            for head in range(heads)
        ] + [
            pl.BlockSpec((block_rows, head_dim), lambda r, dst: (r, 0)),
            pl.BlockSpec((block_rows, head_dim), lambda r, dst: (r, 0)),
            pl.BlockSpec((ext_rows, head_dim), lambda r, dst: (0, 0)),
            pl.BlockSpec((ext_rows, head_dim), lambda r, dst: (0, 0)),
            pl.BlockSpec((1, block_rows, 1), lambda r, dst: (r, 0, 0)),
        ],
        out_specs=pl.BlockSpec((1, block_rows, width), lambda r, dst: (dst[r], 0, 0)),
    )
    return pl.pallas_call(
        kernel,
        grid_spec=grid_spec,
        out_shape=jax.ShapeDtypeStruct((n_dest, block_rows, width), q.dtype),
        cost_estimate=pl.CostEstimate(
            flops=flops,
            transcendentals=per_dev * heads * block_rows * span,
            bytes_accessed=2 * rows * width * 2
            + 2 * ext_rows * head_dim * 2,
        ),
    )(dest, *([q] * heads), cos_t, sin_t, k_ext, v_ext, lo)


def local(queries, keys, values, rope_factors, doc_lengths, owner_map):
    ctx_size = lax.axis_size("ctx")
    ctx_index = lax.axis_index("ctx")
    tp_size = lax.axis_size("tp")
    row_count = queries.shape[0]
    per_dev = owner_map.shape[1]
    block_rows = row_count // per_dev
    tail_rows = row_count // 4
    span = tail_rows + block_rows
    head_dim = 2 * rope_factors.shape[0]
    kv_heads = keys.shape[1] // head_dim
    kv_local = kv_heads // tp_size
    shard_rows = keys.shape[0]

    kv = jnp.stack(
        [
            keys.reshape(shard_rows, tp_size, kv_local * head_dim),
            values.reshape(shard_rows, tp_size, kv_local * head_dim),
        ],
        axis=2,
    ).reshape(shard_rows, tp_size * 2 * kv_local * head_dim)
    kv = lax.all_to_all(kv, "tp", split_axis=1, concat_axis=0, tiled=True)
    kv_tail = passed_along(kv[row_count - tail_rows :], "ctx", 1)
    kv_ext = jnp.concatenate([kv_tail, kv], axis=0)
    kv_width = kv_local * head_dim
    k_raw = kv_ext[:, :kv_width]
    v_ext = kv_ext[:, kv_width:]

    ext_rows = row_count + tail_rows
    pos_ext = ctx_index * row_count - tail_rows + jnp.arange(ext_rows, dtype=jnp.int32)
    doc_ext, off_ext = doc_tables(doc_lengths, pos_ext)
    doc_ext = jnp.where(pos_ext >= 0, doc_ext, -1)
    inverse = inverse_freqs(rope_factors, head_dim)
    cos_ext, sin_ext = rotation_tables(off_ext, inverse, tail_rows)
    k_f = k_raw.astype(jnp.float32)
    k_ext = (k_f * cos_ext + jnp.roll(k_f, head_dim // 2, axis=1) * sin_ext).astype(jnp.bfloat16)
    cos_t = cos_ext[tail_rows:]
    sin_t = sin_ext[tail_rows:]

    lo = (tail_rows + jnp.arange(row_count, dtype=jnp.int32) % block_rows - off_ext[tail_rows:])
    lo = lo.reshape(per_dev, block_rows, 1)

    devices = jnp.arange(ctx_size, dtype=jnp.int32)
    owner_row = lax.dynamic_index_in_dim(owner_map, ctx_index, 0, keepdims=False)

    q_heads = queries.shape[1] // head_dim
    sizes = [2, 2, 2, 2] if q_heads == 8 else [q_heads]
    arrived = []
    first = 0
    for heads in sizes:
        send = attend(
            owner_row, queries, cos_t, sin_t, k_ext, v_ext, lo, ctx_size, head_dim, first, heads
        )
        arrived.append(lax.all_to_all(send, "ctx", split_axis=0, concat_axis=0, tiled=True))
        first += heads

    sources_match = owner_map == ctx_index
    my_sources = jnp.sum(
        jnp.where(sources_match, devices[:, None], 0), axis=0, dtype=jnp.int32
    )
    finished = jnp.concatenate(
        [jnp.take(a, my_sources, axis=0, mode="clip") for a in arrived], axis=-1
    )
    return finished.reshape(row_count, queries.shape[1])


def solution(mesh):
    in_specs = (P("ctx", "tp"), P(("ctx", "tp"), None), P(("ctx", "tp"), None), P(), P(), P())
    out_specs = P("ctx", "tp")
    return jax.shard_map(local, mesh=mesh, in_specs=in_specs, out_specs=out_specs, check_vma=False)
```

```python
import functools
import math

import jax
import jax.numpy as jnp
from jax import lax
from jax.experimental import pallas as pl
from jax.experimental.pallas import tpu as pltpu
from jax.sharding import PartitionSpec as P

THETA = 500000.0


def passed_along(shard, axis, by):
    length = lax.axis_size(axis)
    pairs = [(i, i + by) for i in range(length) if 0 <= i + by < length]
    return lax.ppermute(shard, axis, pairs)


def doc_tables(lengths, positions):
    doc_ends = jnp.cumsum(lengths, dtype=jnp.int32)
    before = positions[:, None] >= doc_ends[None, :]
    doc_index = jnp.sum(before.astype(jnp.int32), axis=1, dtype=jnp.int32)
    doc_start = jnp.sum(jnp.where(before, lengths[None, :], 0), axis=1, dtype=jnp.int32)
    return (doc_index, positions - doc_start)


def inverse_freqs(factors, head_dim):
    half_dim = head_dim // 2
    exponent = jnp.arange(half_dim, dtype=jnp.float32) * (2.0 / head_dim)
    return 1.0 / (factors * jnp.power(jnp.float32(THETA), exponent))


def rotation_tables(offsets, inverse, distinct):
    angles = jnp.arange(distinct, dtype=jnp.int32).astype(jnp.float32)[:, None] * inverse[None, :]
    cosine = jnp.cos(angles)
    sine = jnp.sin(angles)
    table = jnp.concatenate([cosine, cosine, -sine, sine], axis=1)
    rows = jnp.take(table, jnp.clip(offsets, 0, distinct - 1), axis=0, mode="clip")
    half = 2 * inverse.shape[0]
    return rows[:, :half], rows[:, half:]


def rotate(vectors, offsets, inverse):
    half_dim = vectors.shape[-1] // 2
    angles = offsets.astype(jnp.float32)[:, None] * inverse[None, :]
    cosine = jnp.cos(angles)
    sine_part = jnp.sin(angles)
    first_half = vectors[..., :half_dim]
    second_half = vectors[..., half_dim:]
    return jnp.concatenate(
        [
            first_half * cosine - second_half * sine_part,
            second_half * cosine + first_half * sine_part,
        ],
        axis=-1,
    )


def attend_kernel(dest_ref, *refs, heads, head_dim, block_rows, span, scale):
    q_refs = refs[:heads]
    cos_ref, sin_ref, k_ref, v_ref, lo_ref, o_ref = refs[heads:]
    r = pl.program_id(0)
    start = pl.multiple_of(r * block_rows, block_rows)
    if True:
        k = k_ref[pl.ds(start, span), :]
        v = v_ref[pl.ds(start, span), :]
        tail = span - block_rows
        lo = lo_ref[0]
        hi = lax.broadcasted_iota(jnp.int32, (block_rows, 1), 0) + tail
        col = lax.broadcasted_iota(jnp.int32, (block_rows, span), 1)
        visible = (col >= lo) & (col <= hi)
        cos = cos_ref[...]
        sin = sin_ref[...]
        for h in range(heads):
            cols = slice(h * head_dim, (h + 1) * head_dim)
            qh = q_refs[h][...].astype(jnp.float32)
            qr = (qh * cos + pltpu.roll(qh, head_dim // 2, 1) * sin).astype(jnp.bfloat16)
            s = lax.dot_general(
                qr, k, (((1,), (1,)), ((), ())), preferred_element_type=jnp.float32
            ) * scale
            s = jnp.where(visible, s, -1e30)
            m = jnp.max(s, axis=1, keepdims=True)
            p = jnp.exp(s - m)
            l = jnp.sum(p, axis=1, keepdims=True)
            o = jnp.dot(p.astype(jnp.bfloat16), v, preferred_element_type=jnp.float32)
            o_ref[0, :, cols] = (o / l).astype(o_ref.dtype)


def attend(dest, q, cos_t, sin_t, k_ext, v_ext, lo, n_dest, head_dim, first, heads):
    rows, all_width = q.shape
    width = heads * head_dim
    per_dev, block_rows, _ = lo.shape
    ext_rows = k_ext.shape[0]
    span = ext_rows - rows + block_rows
    kernel = functools.partial(
        attend_kernel,
        heads=heads,
        head_dim=head_dim,
        block_rows=block_rows,
        span=span,
        scale=1.0 / math.sqrt(head_dim),
    )
    flops = 4 * per_dev * heads * block_rows * span * head_dim
    grid_spec = pltpu.PrefetchScalarGridSpec(
        num_scalar_prefetch=1,
        grid=(per_dev,),
        in_specs=[
            pl.BlockSpec((block_rows, head_dim), functools.partial(
                lambda r, dst, col: (r, col), col=first + head))
            for head in range(heads)
        ] + [
            pl.BlockSpec((block_rows, head_dim), lambda r, dst: (r, 0)),
            pl.BlockSpec((block_rows, head_dim), lambda r, dst: (r, 0)),
            pl.BlockSpec((ext_rows, head_dim), lambda r, dst: (0, 0)),
            pl.BlockSpec((ext_rows, head_dim), lambda r, dst: (0, 0)),
            pl.BlockSpec((1, block_rows, 1), lambda r, dst: (r, 0, 0)),
        ],
        out_specs=pl.BlockSpec((1, block_rows, width), lambda r, dst: (dst[r], 0, 0)),
    )
    return pl.pallas_call(
        kernel,
        grid_spec=grid_spec,
        out_shape=jax.ShapeDtypeStruct((n_dest, block_rows, width), q.dtype),
        cost_estimate=pl.CostEstimate(
            flops=flops,
            transcendentals=per_dev * heads * block_rows * span,
            bytes_accessed=2 * rows * width * 2
            + 2 * ext_rows * head_dim * 2,
        ),
    )(dest, *([q] * heads), cos_t, sin_t, k_ext, v_ext, lo)


def local(queries, keys, values, rope_factors, doc_lengths, owner_map):
    ctx_size = lax.axis_size("ctx")
    ctx_index = lax.axis_index("ctx")
    tp_size = lax.axis_size("tp")
    row_count = queries.shape[0]
    per_dev = owner_map.shape[1]
    block_rows = row_count // per_dev
    tail_rows = row_count // 4
    span = tail_rows + block_rows
    head_dim = 2 * rope_factors.shape[0]
    kv_heads = keys.shape[1] // head_dim
    kv_local = kv_heads // tp_size
    shard_rows = keys.shape[0]

    kv = jnp.stack(
        [
            keys.reshape(shard_rows, tp_size, kv_local * head_dim),
            values.reshape(shard_rows, tp_size, kv_local * head_dim),
        ],
        axis=2,
    ).reshape(shard_rows, tp_size * 2 * kv_local * head_dim)
    kv = lax.all_to_all(kv, "tp", split_axis=1, concat_axis=0, tiled=True)
    kv_tail = passed_along(kv[row_count - tail_rows :], "ctx", 1)
    kv_ext = jnp.concatenate([kv_tail, kv], axis=0)
    kv_width = kv_local * head_dim
    k_raw = kv_ext[:, :kv_width]
    v_ext = kv_ext[:, kv_width:]

    ext_rows = row_count + tail_rows
    pos_ext = ctx_index * row_count - tail_rows + jnp.arange(ext_rows, dtype=jnp.int32)
    doc_ext, off_ext = doc_tables(doc_lengths, pos_ext)
    doc_ext = jnp.where(pos_ext >= 0, doc_ext, -1)
    inverse = inverse_freqs(rope_factors, head_dim)
    cos_ext, sin_ext = rotation_tables(off_ext, inverse, tail_rows)
    k_f = k_raw.astype(jnp.float32)
    k_ext = (k_f * cos_ext + jnp.roll(k_f, head_dim // 2, axis=1) * sin_ext).astype(jnp.bfloat16)
    cos_t = cos_ext[tail_rows:]
    sin_t = sin_ext[tail_rows:]

    lo = (tail_rows + jnp.arange(row_count, dtype=jnp.int32) % block_rows - off_ext[tail_rows:])
    lo = lo.reshape(per_dev, block_rows, 1)

    devices = jnp.arange(ctx_size, dtype=jnp.int32)
    owner_row = lax.dynamic_index_in_dim(owner_map, ctx_index, 0, keepdims=False)

    q_heads = queries.shape[1] // head_dim
    sizes = [2, 2, 2, 2] if q_heads == 8 else [q_heads]
    arrived = []
    first = 0
    for heads in sizes:
        send = attend(
            owner_row, queries, cos_t, sin_t, k_ext, v_ext, lo, ctx_size, head_dim, first, heads
        )
        arrived.append(lax.all_to_all(send, "ctx", split_axis=0, concat_axis=0, tiled=True))
        first += heads

    sources_match = owner_map == ctx_index
    my_sources = jnp.sum(
        jnp.where(sources_match, devices[:, None], 0), axis=0, dtype=jnp.int32
    )
    finished = jnp.zeros((per_dev, block_rows, queries.shape[1]), queries.dtype)
    first = 0
    for heads, a in zip(sizes, arrived):
        finished = lax.dynamic_update_slice(
            finished, jnp.take(a, my_sources, axis=0, mode="clip"), (0, 0, first * head_dim)
        )
        first += heads
    return finished.reshape(row_count, queries.shape[1])


def solution(mesh):
    in_specs = (P("ctx", "tp"), P(("ctx", "tp"), None), P(("ctx", "tp"), None), P(), P(), P())
    out_specs = P("ctx", "tp")
    return jax.shard_map(local, mesh=mesh, in_specs=in_specs, out_specs=out_specs, check_vma=False)
```

```python
import functools
import math

import jax
import jax.numpy as jnp
from jax import lax
from jax.experimental import pallas as pl
from jax.experimental.pallas import tpu as pltpu
from jax.sharding import PartitionSpec as P

THETA = 500000.0


def passed_along(shard, axis, by):
    length = lax.axis_size(axis)
    pairs = [(i, i + by) for i in range(length) if 0 <= i + by < length]
    return lax.ppermute(shard, axis, pairs)


def doc_tables(lengths, positions):
    doc_ends = jnp.cumsum(lengths, dtype=jnp.int32)
    before = positions[:, None] >= doc_ends[None, :]
    doc_index = jnp.sum(before.astype(jnp.int32), axis=1, dtype=jnp.int32)
    doc_start = jnp.sum(jnp.where(before, lengths[None, :], 0), axis=1, dtype=jnp.int32)
    return (doc_index, positions - doc_start)


def inverse_freqs(factors, head_dim):
    half_dim = head_dim // 2
    exponent = jnp.arange(half_dim, dtype=jnp.float32) * (2.0 / head_dim)
    return 1.0 / (factors * jnp.power(jnp.float32(THETA), exponent))


def rotation_tables(offsets, inverse, distinct):
    angles = jnp.arange(distinct, dtype=jnp.int32).astype(jnp.float32)[:, None] * inverse[None, :]
    cosine = jnp.cos(angles)
    sine = jnp.sin(angles)
    table = jnp.concatenate([cosine, cosine, -sine, sine], axis=1)
    rows = jnp.take(table, jnp.clip(offsets, 0, distinct - 1), axis=0, mode="clip")
    half = 2 * inverse.shape[0]
    return rows[:, :half], rows[:, half:]


def rotate(vectors, offsets, inverse):
    half_dim = vectors.shape[-1] // 2
    angles = offsets.astype(jnp.float32)[:, None] * inverse[None, :]
    cosine = jnp.cos(angles)
    sine_part = jnp.sin(angles)
    first_half = vectors[..., :half_dim]
    second_half = vectors[..., half_dim:]
    return jnp.concatenate(
        [
            first_half * cosine - second_half * sine_part,
            second_half * cosine + first_half * sine_part,
        ],
        axis=-1,
    )


def attend_kernel(dest_ref, *refs, heads, head_dim, block_rows, span, scale):
    q_refs = refs[:heads]
    cos_ref, sin_ref, k_ref, v_ref, lo_ref, o_ref = refs[heads:]
    r = pl.program_id(0)
    start = pl.multiple_of(r * block_rows, block_rows)
    if True:
        k = k_ref[pl.ds(start, span), :]
        v = v_ref[pl.ds(start, span), :]
        tail = span - block_rows
        lo = lo_ref[0]
        hi = lax.broadcasted_iota(jnp.int32, (block_rows, 1), 0) + tail
        col = lax.broadcasted_iota(jnp.int32, (block_rows, span), 1)
        visible = (col >= lo) & (col <= hi)
        cos = cos_ref[...]
        sin = sin_ref[...]
        for h in range(heads):
            cols = slice(h * head_dim, (h + 1) * head_dim)
            qh = q_refs[h][...].astype(jnp.float32)
            qr = (qh * cos + pltpu.roll(qh, head_dim // 2, 1) * sin).astype(jnp.bfloat16)
            s = lax.dot_general(
                qr, k, (((1,), (1,)), ((), ())), preferred_element_type=jnp.float32
            ) * scale
            s = jnp.where(visible, s, -1e30)
            m = jnp.max(s, axis=1, keepdims=True)
            p = jnp.exp(s - m)
            l = jnp.sum(p, axis=1, keepdims=True)
            o = jnp.dot(p.astype(jnp.bfloat16), v, preferred_element_type=jnp.float32)
            o_ref[0, :, cols] = (o / l).astype(o_ref.dtype)


def attend(dest, q, cos_t, sin_t, k_ext, v_ext, lo, n_dest, head_dim, first, heads):
    rows, all_width = q.shape
    width = heads * head_dim
    per_dev, block_rows, _ = lo.shape
    ext_rows = k_ext.shape[0]
    span = ext_rows - rows + block_rows
    kernel = functools.partial(
        attend_kernel,
        heads=heads,
        head_dim=head_dim,
        block_rows=block_rows,
        span=span,
        scale=1.0 / math.sqrt(head_dim),
    )
    flops = 4 * per_dev * heads * block_rows * span * head_dim
    grid_spec = pltpu.PrefetchScalarGridSpec(
        num_scalar_prefetch=1,
        grid=(per_dev,),
        in_specs=[
            pl.BlockSpec((block_rows, head_dim), functools.partial(
                lambda r, dst, col: (r, col), col=first + head))
            for head in range(heads)
        ] + [
            pl.BlockSpec((block_rows, head_dim), lambda r, dst: (r, 0)),
            pl.BlockSpec((block_rows, head_dim), lambda r, dst: (r, 0)),
            pl.BlockSpec((ext_rows, head_dim), lambda r, dst: (0, 0)),
            pl.BlockSpec((ext_rows, head_dim), lambda r, dst: (0, 0)),
            pl.BlockSpec((1, block_rows, 1), lambda r, dst: (r, 0, 0)),
        ],
        out_specs=pl.BlockSpec((1, block_rows, width), lambda r, dst: (dst[r], 0, 0)),
    )
    return pl.pallas_call(
        kernel,
        grid_spec=grid_spec,
        out_shape=jax.ShapeDtypeStruct((n_dest, block_rows, width), q.dtype),
        cost_estimate=pl.CostEstimate(
            flops=flops,
            transcendentals=per_dev * heads * block_rows * span,
            bytes_accessed=2 * rows * width * 2
            + 2 * ext_rows * head_dim * 2,
        ),
    )(dest, *([q] * heads), cos_t, sin_t, k_ext, v_ext, lo)


def local(queries, keys, values, rope_factors, doc_lengths, owner_map):
    ctx_size = lax.axis_size("ctx")
    ctx_index = lax.axis_index("ctx")
    tp_size = lax.axis_size("tp")
    row_count = queries.shape[0]
    per_dev = owner_map.shape[1]
    block_rows = row_count // per_dev
    tail_rows = row_count // 4
    span = tail_rows + block_rows
    head_dim = 2 * rope_factors.shape[0]
    kv_heads = keys.shape[1] // head_dim
    kv_local = kv_heads // tp_size
    shard_rows = keys.shape[0]

    kv = jnp.stack(
        [
            keys.reshape(shard_rows, tp_size, kv_local * head_dim),
            values.reshape(shard_rows, tp_size, kv_local * head_dim),
        ],
        axis=2,
    ).reshape(shard_rows, tp_size * 2 * kv_local * head_dim)
    kv = lax.all_to_all(kv, "tp", split_axis=1, concat_axis=0, tiled=True)
    kv_tail = passed_along(kv[row_count - tail_rows :], "ctx", 1)
    kv_ext = jnp.concatenate([kv_tail, kv], axis=0)
    kv_width = kv_local * head_dim
    k_raw = kv_ext[:, :kv_width]
    v_ext = kv_ext[:, kv_width:]

    ext_rows = row_count + tail_rows
    pos_ext = ctx_index * row_count - tail_rows + jnp.arange(ext_rows, dtype=jnp.int32)
    doc_ext, off_ext = doc_tables(doc_lengths, pos_ext)
    doc_ext = jnp.where(pos_ext >= 0, doc_ext, -1)
    inverse = inverse_freqs(rope_factors, head_dim)
    cos_ext, sin_ext = rotation_tables(off_ext, inverse, tail_rows)
    k_f = k_raw.astype(jnp.float32)
    k_ext = (k_f * cos_ext + jnp.roll(k_f, head_dim // 2, axis=1) * sin_ext).astype(jnp.bfloat16)
    cos_t = cos_ext[tail_rows:]
    sin_t = sin_ext[tail_rows:]

    lo = (tail_rows + jnp.arange(row_count, dtype=jnp.int32) % block_rows - off_ext[tail_rows:])
    lo = lo.reshape(per_dev, block_rows, 1)

    devices = jnp.arange(ctx_size, dtype=jnp.int32)
    owner_row = lax.dynamic_index_in_dim(owner_map, ctx_index, 0, keepdims=False)

    q_heads = queries.shape[1] // head_dim
    sizes = [2, 3, 3] if q_heads == 8 else [q_heads]
    arrived = []
    first = 0
    for heads in sizes:
        send = attend(
            owner_row, queries, cos_t, sin_t, k_ext, v_ext, lo, ctx_size, head_dim, first, heads
        )
        arrived.append(lax.all_to_all(send, "ctx", split_axis=0, concat_axis=0, tiled=True))
        first += heads

    sources_match = owner_map == ctx_index
    my_sources = jnp.sum(
        jnp.where(sources_match, devices[:, None], 0), axis=0, dtype=jnp.int32
    )
    finished = jnp.zeros((per_dev, block_rows, queries.shape[1]), queries.dtype)
    first = 0
    for heads, a in zip(sizes, arrived):
        finished = lax.dynamic_update_slice(
            finished, jnp.take(a, my_sources, axis=0, mode="clip"), (0, 0, first * head_dim)
        )
        first += heads
    return finished.reshape(row_count, queries.shape[1])


def solution(mesh):
    in_specs = (P("ctx", "tp"), P(("ctx", "tp"), None), P(("ctx", "tp"), None), P(), P(), P())
    out_specs = P("ctx", "tp")
    return jax.shard_map(local, mesh=mesh, in_specs=in_specs, out_specs=out_specs, check_vma=False)
```

```python
import functools
import math

import jax
import jax.numpy as jnp
from jax import lax
from jax.experimental import pallas as pl
from jax.experimental.pallas import tpu as pltpu
from jax.sharding import PartitionSpec as P

THETA = 500000.0


def passed_along(shard, axis, by):
    length = lax.axis_size(axis)
    pairs = [(i, i + by) for i in range(length) if 0 <= i + by < length]
    return lax.ppermute(shard, axis, pairs)


def doc_tables(lengths, positions):
    doc_ends = jnp.cumsum(lengths, dtype=jnp.int32)
    before = positions[:, None] >= doc_ends[None, :]
    doc_index = jnp.sum(before.astype(jnp.int32), axis=1, dtype=jnp.int32)
    doc_start = jnp.sum(jnp.where(before, lengths[None, :], 0), axis=1, dtype=jnp.int32)
    return (doc_index, positions - doc_start)


def inverse_freqs(factors, head_dim):
    half_dim = head_dim // 2
    exponent = jnp.arange(half_dim, dtype=jnp.float32) * (2.0 / head_dim)
    return 1.0 / (factors * jnp.power(jnp.float32(THETA), exponent))


def rotation_tables(offsets, inverse, distinct):
    angles = jnp.arange(distinct, dtype=jnp.int32).astype(jnp.float32)[:, None] * inverse[None, :]
    cosine = jnp.cos(angles)
    sine = jnp.sin(angles)
    table = jnp.concatenate([cosine, cosine, -sine, sine], axis=1)
    rows = jnp.take(table, jnp.clip(offsets, 0, distinct - 1), axis=0, mode="clip")
    half = 2 * inverse.shape[0]
    return rows[:, :half], rows[:, half:]


def rotate(vectors, offsets, inverse):
    half_dim = vectors.shape[-1] // 2
    angles = offsets.astype(jnp.float32)[:, None] * inverse[None, :]
    cosine = jnp.cos(angles)
    sine_part = jnp.sin(angles)
    first_half = vectors[..., :half_dim]
    second_half = vectors[..., half_dim:]
    return jnp.concatenate(
        [
            first_half * cosine - second_half * sine_part,
            second_half * cosine + first_half * sine_part,
        ],
        axis=-1,
    )


def attend_kernel(dest_ref, *refs, heads, head_dim, block_rows, span, scale):
    q_refs = refs[:heads]
    cos_ref, sin_ref, k_ref, v_ref, lo_ref, o_ref = refs[heads:]
    r = pl.program_id(0)
    start = pl.multiple_of(r * block_rows, block_rows)
    if True:
        k = k_ref[pl.ds(start, span), :]
        v = v_ref[pl.ds(start, span), :]
        tail = span - block_rows
        lo = lo_ref[0]
        hi = lax.broadcasted_iota(jnp.int32, (block_rows, 1), 0) + tail
        col = lax.broadcasted_iota(jnp.int32, (block_rows, span), 1)
        visible = (col >= lo) & (col <= hi)
        cos = cos_ref[...]
        sin = sin_ref[...]
        for h in range(heads):
            cols = slice(h * head_dim, (h + 1) * head_dim)
            qh = q_refs[h][...].astype(jnp.float32)
            qr = (qh * cos + pltpu.roll(qh, head_dim // 2, 1) * sin).astype(jnp.bfloat16)
            s = lax.dot_general(
                qr, k, (((1,), (1,)), ((), ())), preferred_element_type=jnp.float32
            ) * scale
            s = jnp.where(visible, s, -1e30)
            m = jnp.max(s, axis=1, keepdims=True)
            p = jnp.exp(s - m)
            l = jnp.sum(p, axis=1, keepdims=True)
            o = jnp.dot(p.astype(jnp.bfloat16), v, preferred_element_type=jnp.float32)
            o_ref[0, :, cols] = (o / l).astype(o_ref.dtype)


def attend(dest, q, cos_t, sin_t, k_ext, v_ext, lo, n_dest, head_dim, first, heads):
    rows, all_width = q.shape
    width = heads * head_dim
    per_dev, block_rows, _ = lo.shape
    ext_rows = k_ext.shape[0]
    span = ext_rows - rows + block_rows
    kernel = functools.partial(
        attend_kernel,
        heads=heads,
        head_dim=head_dim,
        block_rows=block_rows,
        span=span,
        scale=1.0 / math.sqrt(head_dim),
    )
    flops = 4 * per_dev * heads * block_rows * span * head_dim
    grid_spec = pltpu.PrefetchScalarGridSpec(
        num_scalar_prefetch=1,
        grid=(per_dev,),
        in_specs=[
            pl.BlockSpec((block_rows, head_dim), functools.partial(
                lambda r, dst, col: (r, col), col=first + head))
            for head in range(heads)
        ] + [
            pl.BlockSpec((block_rows, head_dim), lambda r, dst: (r, 0)),
            pl.BlockSpec((block_rows, head_dim), lambda r, dst: (r, 0)),
            pl.BlockSpec((ext_rows, head_dim), lambda r, dst: (0, 0)),
            pl.BlockSpec((ext_rows, head_dim), lambda r, dst: (0, 0)),
            pl.BlockSpec((1, block_rows, 1), lambda r, dst: (r, 0, 0)),
        ],
        out_specs=pl.BlockSpec((1, block_rows, width), lambda r, dst: (dst[r], 0, 0)),
    )
    return pl.pallas_call(
        kernel,
        grid_spec=grid_spec,
        out_shape=jax.ShapeDtypeStruct((n_dest, block_rows, width), q.dtype),
        cost_estimate=pl.CostEstimate(
            flops=flops,
            transcendentals=per_dev * heads * block_rows * span,
            bytes_accessed=2 * rows * width * 2
            + 2 * ext_rows * head_dim * 2,
        ),
    )(dest, *([q] * heads), cos_t, sin_t, k_ext, v_ext, lo)


def local(queries, keys, values, rope_factors, doc_lengths, owner_map):
    ctx_size = lax.axis_size("ctx")
    ctx_index = lax.axis_index("ctx")
    tp_size = lax.axis_size("tp")
    row_count = queries.shape[0]
    per_dev = owner_map.shape[1]
    block_rows = row_count // per_dev
    tail_rows = row_count // 4
    span = tail_rows + block_rows
    head_dim = 2 * rope_factors.shape[0]
    kv_heads = keys.shape[1] // head_dim
    kv_local = kv_heads // tp_size
    shard_rows = keys.shape[0]

    kv = jnp.stack(
        [
            keys.reshape(shard_rows, tp_size, kv_local * head_dim),
            values.reshape(shard_rows, tp_size, kv_local * head_dim),
        ],
        axis=2,
    ).reshape(shard_rows, tp_size * 2 * kv_local * head_dim)
    kv = lax.all_to_all(kv, "tp", split_axis=1, concat_axis=0, tiled=True)
    kv_tail = passed_along(kv[row_count - tail_rows :], "ctx", 1)
    kv_ext = jnp.concatenate([kv_tail, kv], axis=0)
    kv_width = kv_local * head_dim
    k_raw = kv_ext[:, :kv_width]
    v_ext = kv_ext[:, kv_width:]

    ext_rows = row_count + tail_rows
    pos_ext = ctx_index * row_count - tail_rows + jnp.arange(ext_rows, dtype=jnp.int32)
    doc_ext, off_ext = doc_tables(doc_lengths, pos_ext)
    doc_ext = jnp.where(pos_ext >= 0, doc_ext, -1)
    inverse = inverse_freqs(rope_factors, head_dim)
    cos_ext, sin_ext = rotation_tables(off_ext, inverse, tail_rows)
    k_f = k_raw.astype(jnp.float32)
    k_ext = (k_f * cos_ext + jnp.roll(k_f, head_dim // 2, axis=1) * sin_ext).astype(jnp.bfloat16)
    cos_t = cos_ext[tail_rows:]
    sin_t = sin_ext[tail_rows:]

    lo = (tail_rows + jnp.arange(row_count, dtype=jnp.int32) % block_rows - off_ext[tail_rows:])
    lo = lo.reshape(per_dev, block_rows, 1)

    devices = jnp.arange(ctx_size, dtype=jnp.int32)
    owner_row = lax.dynamic_index_in_dim(owner_map, ctx_index, 0, keepdims=False)

    q_heads = queries.shape[1] // head_dim
    sizes = [2, 6] if q_heads == 8 else [q_heads]
    arrived = []
    first = 0
    for heads in sizes:
        send = attend(
            owner_row, queries, cos_t, sin_t, k_ext, v_ext, lo, ctx_size, head_dim, first, heads
        )
        arrived.append(lax.all_to_all(send, "ctx", split_axis=0, concat_axis=0, tiled=True))
        first += heads

    sources_match = owner_map == ctx_index
    my_sources = jnp.sum(
        jnp.where(sources_match, devices[:, None], 0), axis=0, dtype=jnp.int32
    )
    finished = jnp.zeros((per_dev, block_rows, queries.shape[1]), queries.dtype)
    first = 0
    for heads, a in zip(sizes, arrived):
        finished = lax.dynamic_update_slice(
            finished, jnp.take(a, my_sources, axis=0, mode="clip"), (0, 0, first * head_dim)
        )
        first += heads
    return finished.reshape(row_count, queries.shape[1])


def solution(mesh):
    in_specs = (P("ctx", "tp"), P(("ctx", "tp"), None), P(("ctx", "tp"), None), P(), P(), P())
    out_specs = P("ctx", "tp")
    return jax.shard_map(local, mesh=mesh, in_specs=in_specs, out_specs=out_specs, check_vma=False)
```

```python
import functools
import math

import jax
import jax.numpy as jnp
from jax import lax
from jax.experimental import pallas as pl
from jax.experimental.pallas import tpu as pltpu
from jax.sharding import PartitionSpec as P

THETA = 500000.0


def passed_along(shard, axis, by):
    length = lax.axis_size(axis)
    pairs = [(i, i + by) for i in range(length) if 0 <= i + by < length]
    return lax.ppermute(shard, axis, pairs)


def doc_tables(lengths, positions):
    doc_ends = jnp.cumsum(lengths, dtype=jnp.int32)
    before = positions[:, None] >= doc_ends[None, :]
    doc_index = jnp.sum(before.astype(jnp.int32), axis=1, dtype=jnp.int32)
    doc_start = jnp.sum(jnp.where(before, lengths[None, :], 0), axis=1, dtype=jnp.int32)
    return (doc_index, positions - doc_start)


def inverse_freqs(factors, head_dim):
    half_dim = head_dim // 2
    exponent = jnp.arange(half_dim, dtype=jnp.float32) * (2.0 / head_dim)
    return 1.0 / (factors * jnp.power(jnp.float32(THETA), exponent))


def rotation_tables(offsets, inverse, distinct):
    angles = jnp.arange(distinct, dtype=jnp.int32).astype(jnp.float32)[:, None] * inverse[None, :]
    cosine = jnp.cos(angles)
    sine = jnp.sin(angles)
    table = jnp.concatenate([cosine, cosine, -sine, sine], axis=1)
    rows = jnp.take(table, jnp.clip(offsets, 0, distinct - 1), axis=0, mode="clip")
    half = 2 * inverse.shape[0]
    return rows[:, :half], rows[:, half:]


def rotate(vectors, offsets, inverse):
    half_dim = vectors.shape[-1] // 2
    angles = offsets.astype(jnp.float32)[:, None] * inverse[None, :]
    cosine = jnp.cos(angles)
    sine_part = jnp.sin(angles)
    first_half = vectors[..., :half_dim]
    second_half = vectors[..., half_dim:]
    return jnp.concatenate(
        [
            first_half * cosine - second_half * sine_part,
            second_half * cosine + first_half * sine_part,
        ],
        axis=-1,
    )


def attend_kernel(dest_ref, *refs, heads, head_dim, block_rows, span, scale):
    q_refs = refs[:heads]
    cos_ref, sin_ref, k_ref, v_ref, lo_ref, o_ref = refs[heads:]
    r = pl.program_id(0)
    start = pl.multiple_of(r * block_rows, block_rows)
    if True:
        k = k_ref[pl.ds(start, span), :]
        v = v_ref[pl.ds(start, span), :]
        tail = span - block_rows
        lo = lo_ref[0]
        hi = lax.broadcasted_iota(jnp.int32, (block_rows, 1), 0) + tail
        col = lax.broadcasted_iota(jnp.int32, (block_rows, span), 1)
        visible = (col >= lo) & (col <= hi)
        cos = cos_ref[...]
        sin = sin_ref[...]
        for h in range(heads):
            cols = slice(h * head_dim, (h + 1) * head_dim)
            qh = q_refs[h][...].astype(jnp.float32)
            qr = (qh * cos + pltpu.roll(qh, head_dim // 2, 1) * sin).astype(jnp.bfloat16)
            s = lax.dot_general(
                qr, k, (((1,), (1,)), ((), ())), preferred_element_type=jnp.float32
            ) * scale
            s = jnp.where(visible, s, -1e30)
            m = jnp.max(s, axis=1, keepdims=True)
            p = jnp.exp(s - m)
            l = jnp.sum(p, axis=1, keepdims=True)
            o = jnp.dot(p.astype(jnp.bfloat16), v, preferred_element_type=jnp.float32)
            o_ref[0, :, cols] = (o / l).astype(o_ref.dtype)


def attend(dest, q, cos_t, sin_t, k_ext, v_ext, lo, n_dest, head_dim, first, heads):
    rows, all_width = q.shape
    width = heads * head_dim
    per_dev, block_rows, _ = lo.shape
    ext_rows = k_ext.shape[0]
    span = ext_rows - rows + block_rows
    kernel = functools.partial(
        attend_kernel,
        heads=heads,
        head_dim=head_dim,
        block_rows=block_rows,
        span=span,
        scale=1.0 / math.sqrt(head_dim),
    )
    flops = 4 * per_dev * heads * block_rows * span * head_dim
    grid_spec = pltpu.PrefetchScalarGridSpec(
        num_scalar_prefetch=1,
        grid=(per_dev,),
        in_specs=[
            pl.BlockSpec((block_rows, head_dim), functools.partial(
                lambda r, dst, col: (r, col), col=first + head))
            for head in range(heads)
        ] + [
            pl.BlockSpec((block_rows, head_dim), lambda r, dst: (r, 0)),
            pl.BlockSpec((block_rows, head_dim), lambda r, dst: (r, 0)),
            pl.BlockSpec((ext_rows, head_dim), lambda r, dst: (0, 0)),
            pl.BlockSpec((ext_rows, head_dim), lambda r, dst: (0, 0)),
            pl.BlockSpec((1, block_rows, 1), lambda r, dst: (r, 0, 0)),
        ],
        out_specs=pl.BlockSpec((1, block_rows, width), lambda r, dst: (dst[r], 0, 0)),
    )
    return pl.pallas_call(
        kernel,
        grid_spec=grid_spec,
        out_shape=jax.ShapeDtypeStruct((n_dest, block_rows, width), q.dtype),
        cost_estimate=pl.CostEstimate(
            flops=flops,
            transcendentals=per_dev * heads * block_rows * span,
            bytes_accessed=2 * rows * width * 2
            + 2 * ext_rows * head_dim * 2,
        ),
    )(dest, *([q] * heads), cos_t, sin_t, k_ext, v_ext, lo)


def local(queries, keys, values, rope_factors, doc_lengths, owner_map):
    ctx_size = lax.axis_size("ctx")
    ctx_index = lax.axis_index("ctx")
    tp_size = lax.axis_size("tp")
    row_count = queries.shape[0]
    per_dev = owner_map.shape[1]
    block_rows = row_count // per_dev
    tail_rows = row_count // 4
    span = tail_rows + block_rows
    head_dim = 2 * rope_factors.shape[0]
    kv_heads = keys.shape[1] // head_dim
    kv_local = kv_heads // tp_size
    shard_rows = keys.shape[0]

    kv = jnp.stack(
        [
            keys.reshape(shard_rows, tp_size, kv_local * head_dim),
            values.reshape(shard_rows, tp_size, kv_local * head_dim),
        ],
        axis=2,
    ).reshape(shard_rows, tp_size * 2 * kv_local * head_dim)
    kv = lax.all_to_all(kv, "tp", split_axis=1, concat_axis=0, tiled=True)
    kv_tail = passed_along(kv[row_count - tail_rows :], "ctx", 1)
    kv_ext = jnp.concatenate([kv_tail, kv], axis=0)
    kv_width = kv_local * head_dim
    k_raw = kv_ext[:, :kv_width]
    v_ext = kv_ext[:, kv_width:]

    ext_rows = row_count + tail_rows
    pos_ext = ctx_index * row_count - tail_rows + jnp.arange(ext_rows, dtype=jnp.int32)
    doc_ext, off_ext = doc_tables(doc_lengths, pos_ext)
    doc_ext = jnp.where(pos_ext >= 0, doc_ext, -1)
    inverse = inverse_freqs(rope_factors, head_dim)
    cos_ext, sin_ext = rotation_tables(off_ext, inverse, tail_rows)
    k_f = k_raw.astype(jnp.float32)
    k_ext = (k_f * cos_ext + jnp.roll(k_f, head_dim // 2, axis=1) * sin_ext).astype(jnp.bfloat16)
    cos_t = cos_ext[tail_rows:]
    sin_t = sin_ext[tail_rows:]

    lo = (tail_rows + jnp.arange(row_count, dtype=jnp.int32) % block_rows - off_ext[tail_rows:])
    lo = lo.reshape(per_dev, block_rows, 1)

    devices = jnp.arange(ctx_size, dtype=jnp.int32)
    owner_row = lax.dynamic_index_in_dim(owner_map, ctx_index, 0, keepdims=False)

    q_heads = queries.shape[1] // head_dim
    sizes = [3, 3, 2] if q_heads == 8 else [q_heads]
    arrived = []
    first = 0
    for heads in sizes:
        send = attend(
            owner_row, queries, cos_t, sin_t, k_ext, v_ext, lo, ctx_size, head_dim, first, heads
        )
        arrived.append(lax.all_to_all(send, "ctx", split_axis=0, concat_axis=0, tiled=True))
        first += heads

    sources_match = owner_map == ctx_index
    my_sources = jnp.sum(
        jnp.where(sources_match, devices[:, None], 0), axis=0, dtype=jnp.int32
    )
    finished = jnp.zeros((per_dev, block_rows, queries.shape[1]), queries.dtype)
    first = 0
    for heads, a in zip(sizes, arrived):
        finished = lax.dynamic_update_slice(
            finished, jnp.take(a, my_sources, axis=0, mode="clip"), (0, 0, first * head_dim)
        )
        first += heads
    return finished.reshape(row_count, queries.shape[1])


def solution(mesh):
    in_specs = (P("ctx", "tp"), P(("ctx", "tp"), None), P(("ctx", "tp"), None), P(), P(), P())
    out_specs = P("ctx", "tp")
    return jax.shard_map(local, mesh=mesh, in_specs=in_specs, out_specs=out_specs, check_vma=False)
```

```python
import functools
import math

import jax
import jax.numpy as jnp
from jax import lax
from jax.experimental import pallas as pl
from jax.experimental.pallas import tpu as pltpu
from jax.sharding import PartitionSpec as P

THETA = 500000.0


def passed_along(shard, axis, by):
    length = lax.axis_size(axis)
    pairs = [(i, i + by) for i in range(length) if 0 <= i + by < length]
    return lax.ppermute(shard, axis, pairs)


def doc_tables(lengths, positions):
    doc_ends = jnp.cumsum(lengths, dtype=jnp.int32)
    before = positions[:, None] >= doc_ends[None, :]
    doc_index = jnp.sum(before.astype(jnp.int32), axis=1, dtype=jnp.int32)
    doc_start = jnp.sum(jnp.where(before, lengths[None, :], 0), axis=1, dtype=jnp.int32)
    return (doc_index, positions - doc_start)


def inverse_freqs(factors, head_dim):
    half_dim = head_dim // 2
    exponent = jnp.arange(half_dim, dtype=jnp.float32) * (2.0 / head_dim)
    return 1.0 / (factors * jnp.power(jnp.float32(THETA), exponent))


def rotation_tables(offsets, inverse, distinct):
    angles = jnp.arange(distinct, dtype=jnp.int32).astype(jnp.float32)[:, None] * inverse[None, :]
    cosine = jnp.cos(angles)
    sine = jnp.sin(angles)
    table = jnp.concatenate([cosine, cosine, -sine, sine], axis=1)
    rows = jnp.take(table, jnp.clip(offsets, 0, distinct - 1), axis=0, mode="clip")
    half = 2 * inverse.shape[0]
    return rows[:, :half], rows[:, half:]


def rotate(vectors, offsets, inverse):
    half_dim = vectors.shape[-1] // 2
    angles = offsets.astype(jnp.float32)[:, None] * inverse[None, :]
    cosine = jnp.cos(angles)
    sine_part = jnp.sin(angles)
    first_half = vectors[..., :half_dim]
    second_half = vectors[..., half_dim:]
    return jnp.concatenate(
        [
            first_half * cosine - second_half * sine_part,
            second_half * cosine + first_half * sine_part,
        ],
        axis=-1,
    )


def attend_kernel(dest_ref, *refs, heads, head_dim, block_rows, span, scale):
    q_refs = refs[:heads]
    cos_ref, sin_ref, k_ref, v_ref, lo_ref, o_ref = refs[heads:]
    r = pl.program_id(0)
    start = pl.multiple_of(r * block_rows, block_rows)
    if True:
        k = k_ref[pl.ds(start, span), :]
        v = v_ref[pl.ds(start, span), :]
        tail = span - block_rows
        lo = lo_ref[0]
        hi = lax.broadcasted_iota(jnp.int32, (block_rows, 1), 0) + tail
        col = lax.broadcasted_iota(jnp.int32, (block_rows, span), 1)
        visible = (col >= lo) & (col <= hi)
        cos = cos_ref[...]
        sin = sin_ref[...]
        for h in range(heads):
            cols = slice(h * head_dim, (h + 1) * head_dim)
            qh = q_refs[h][...].astype(jnp.float32)
            qr = (qh * cos + pltpu.roll(qh, head_dim // 2, 1) * sin).astype(jnp.bfloat16)
            s = lax.dot_general(
                qr, k, (((1,), (1,)), ((), ())), preferred_element_type=jnp.float32
            ) * scale
            s = jnp.where(visible, s, -1e30)
            m = jnp.max(s, axis=1, keepdims=True)
            p = jnp.exp(s - m)
            l = jnp.sum(p, axis=1, keepdims=True)
            o = jnp.dot(p.astype(jnp.bfloat16), v, preferred_element_type=jnp.float32)
            o_ref[0, :, cols] = (o / l).astype(o_ref.dtype)


def attend(dest, q, cos_t, sin_t, k_ext, v_ext, lo, n_dest, head_dim, first, heads):
    rows, all_width = q.shape
    width = heads * head_dim
    per_dev, block_rows, _ = lo.shape
    ext_rows = k_ext.shape[0]
    span = ext_rows - rows + block_rows
    kernel = functools.partial(
        attend_kernel,
        heads=heads,
        head_dim=head_dim,
        block_rows=block_rows,
        span=span,
        scale=1.0 / math.sqrt(head_dim),
    )
    flops = 4 * per_dev * heads * block_rows * span * head_dim
    grid_spec = pltpu.PrefetchScalarGridSpec(
        num_scalar_prefetch=1,
        grid=(per_dev,),
        in_specs=[
            pl.BlockSpec((block_rows, head_dim), functools.partial(
                lambda r, dst, col: (r, col), col=first + head))
            for head in range(heads)
        ] + [
            pl.BlockSpec((block_rows, head_dim), lambda r, dst: (r, 0)),
            pl.BlockSpec((block_rows, head_dim), lambda r, dst: (r, 0)),
            pl.BlockSpec((ext_rows, head_dim), lambda r, dst: (0, 0)),
            pl.BlockSpec((ext_rows, head_dim), lambda r, dst: (0, 0)),
            pl.BlockSpec((1, block_rows, 1), lambda r, dst: (r, 0, 0)),
        ],
        out_specs=pl.BlockSpec((1, block_rows, width), lambda r, dst: (dst[r], 0, 0)),
    )
    return pl.pallas_call(
        kernel,
        grid_spec=grid_spec,
        out_shape=jax.ShapeDtypeStruct((n_dest, block_rows, width), q.dtype),
        cost_estimate=pl.CostEstimate(
            flops=flops,
            transcendentals=per_dev * heads * block_rows * span,
            bytes_accessed=2 * rows * width * 2
            + 2 * ext_rows * head_dim * 2,
        ),
    )(dest, *([q] * heads), cos_t, sin_t, k_ext, v_ext, lo)


def local(queries, keys, values, rope_factors, doc_lengths, owner_map):
    ctx_size = lax.axis_size("ctx")
    ctx_index = lax.axis_index("ctx")
    tp_size = lax.axis_size("tp")
    row_count = queries.shape[0]
    per_dev = owner_map.shape[1]
    block_rows = row_count // per_dev
    tail_rows = row_count // 4
    span = tail_rows + block_rows
    head_dim = 2 * rope_factors.shape[0]
    kv_heads = keys.shape[1] // head_dim
    kv_local = kv_heads // tp_size
    shard_rows = keys.shape[0]

    kv_width = kv_local * head_dim
    kv = jnp.concatenate(
        [
            keys.reshape(shard_rows, tp_size, kv_width).transpose(1, 0, 2),
            values.reshape(shard_rows, tp_size, kv_width).transpose(1, 0, 2),
        ],
        axis=2,
    )
    kv = lax.all_to_all(kv, "tp", split_axis=0, concat_axis=0, tiled=True)
    kv = kv.reshape(row_count, 2 * kv_width)
    kv_tail = passed_along(kv[row_count - tail_rows :], "ctx", 1)
    kv_ext = jnp.concatenate([kv_tail, kv], axis=0)
    k_raw = kv_ext[:, :kv_width]
    v_ext = kv_ext[:, kv_width:]

    ext_rows = row_count + tail_rows
    pos_ext = ctx_index * row_count - tail_rows + jnp.arange(ext_rows, dtype=jnp.int32)
    doc_ext, off_ext = doc_tables(doc_lengths, pos_ext)
    doc_ext = jnp.where(pos_ext >= 0, doc_ext, -1)
    inverse = inverse_freqs(rope_factors, head_dim)
    cos_ext, sin_ext = rotation_tables(off_ext, inverse, tail_rows)
    k_f = k_raw.astype(jnp.float32)
    k_ext = (k_f * cos_ext + jnp.roll(k_f, head_dim // 2, axis=1) * sin_ext).astype(jnp.bfloat16)
    cos_t = cos_ext[tail_rows:]
    sin_t = sin_ext[tail_rows:]

    lo = (tail_rows + jnp.arange(row_count, dtype=jnp.int32) % block_rows - off_ext[tail_rows:])
    lo = lo.reshape(per_dev, block_rows, 1)

    devices = jnp.arange(ctx_size, dtype=jnp.int32)
    owner_row = lax.dynamic_index_in_dim(owner_map, ctx_index, 0, keepdims=False)

    q_heads = queries.shape[1] // head_dim
    sizes = [2, 3, 3] if q_heads == 8 else [q_heads]
    arrived = []
    first = 0
    for heads in sizes:
        send = attend(
            owner_row, queries, cos_t, sin_t, k_ext, v_ext, lo, ctx_size, head_dim, first, heads
        )
        arrived.append(lax.all_to_all(send, "ctx", split_axis=0, concat_axis=0, tiled=True))
        first += heads

    sources_match = owner_map == ctx_index
    my_sources = jnp.sum(
        jnp.where(sources_match, devices[:, None], 0), axis=0, dtype=jnp.int32
    )
    finished = jnp.zeros((per_dev, block_rows, queries.shape[1]), queries.dtype)
    first = 0
    for heads, a in zip(sizes, arrived):
        finished = lax.dynamic_update_slice(
            finished, jnp.take(a, my_sources, axis=0, mode="clip"), (0, 0, first * head_dim)
        )
        first += heads
    return finished.reshape(row_count, queries.shape[1])


def solution(mesh):
    in_specs = (P("ctx", "tp"), P(("ctx", "tp"), None), P(("ctx", "tp"), None), P(), P(), P())
    out_specs = P("ctx", "tp")
    return jax.shard_map(local, mesh=mesh, in_specs=in_specs, out_specs=out_specs, check_vma=False)
```

```python
import functools
import math

import jax
import jax.numpy as jnp
from jax import lax
from jax.experimental import pallas as pl
from jax.experimental.pallas import tpu as pltpu
from jax.sharding import PartitionSpec as P

THETA = 500000.0


def passed_along(shard, axis, by):
    length = lax.axis_size(axis)
    pairs = [(i, i + by) for i in range(length) if 0 <= i + by < length]
    return lax.ppermute(shard, axis, pairs)


def doc_tables(lengths, positions):
    doc_ends = jnp.cumsum(lengths, dtype=jnp.int32)
    before = positions[:, None] >= doc_ends[None, :]
    doc_index = jnp.sum(before.astype(jnp.int32), axis=1, dtype=jnp.int32)
    doc_start = jnp.sum(jnp.where(before, lengths[None, :], 0), axis=1, dtype=jnp.int32)
    return (doc_index, positions - doc_start)


def inverse_freqs(factors, head_dim):
    half_dim = head_dim // 2
    exponent = jnp.arange(half_dim, dtype=jnp.float32) * (2.0 / head_dim)
    return 1.0 / (factors * jnp.power(jnp.float32(THETA), exponent))


def rotation_rows(offsets, inverse, distinct):
    angles = jnp.arange(distinct, dtype=jnp.int32).astype(jnp.float32)[:, None] * inverse[None, :]
    cosine = jnp.cos(angles)
    sine = jnp.sin(angles)
    table = jnp.concatenate([cosine, cosine, -sine, sine], axis=1)
    return jnp.take(table, jnp.clip(offsets, 0, distinct - 1), axis=0, mode="clip")


def rotate(vectors, offsets, inverse):
    half_dim = vectors.shape[-1] // 2
    angles = offsets.astype(jnp.float32)[:, None] * inverse[None, :]
    cosine = jnp.cos(angles)
    sine_part = jnp.sin(angles)
    first_half = vectors[..., :half_dim]
    second_half = vectors[..., half_dim:]
    return jnp.concatenate(
        [
            first_half * cosine - second_half * sine_part,
            second_half * cosine + first_half * sine_part,
        ],
        axis=-1,
    )


def attend_kernel(
    dest_ref, *refs, heads, head_dim, block_rows, span, scale, first_block, key_base, aliased
):
    q_refs = refs[:heads]
    cos_ref, sin_ref, k_ref, v_ref, lo_ref = refs[heads : heads + 5]
    o_ref = refs[-1]
    r = pl.program_id(0) + first_block
    start = pl.multiple_of(r * block_rows - key_base, block_rows)
    k = k_ref[pl.ds(start, span), :]
    v = v_ref[pl.ds(start, span), :]
    tail = span - block_rows
    lo = lo_ref[0]
    hi = lax.broadcasted_iota(jnp.int32, (block_rows, 1), 0) + tail
    col = lax.broadcasted_iota(jnp.int32, (block_rows, span), 1)
    visible = (col >= lo) & (col <= hi)
    cos = cos_ref[...]
    sin = sin_ref[...]
    for h in range(heads):
        cols = slice(h * head_dim, (h + 1) * head_dim)
        qh = q_refs[h][...].astype(jnp.float32)
        qr = (qh * cos + pltpu.roll(qh, head_dim // 2, 1) * sin).astype(jnp.bfloat16)
        s = lax.dot_general(
            qr, k, (((1,), (1,)), ((), ())), preferred_element_type=jnp.float32
        ) * scale
        s = jnp.where(visible, s, -1e30)
        m = jnp.max(s, axis=1, keepdims=True)
        p = jnp.exp(s - m)
        l = jnp.sum(p, axis=1, keepdims=True)
        o = jnp.dot(p.astype(jnp.bfloat16), v, preferred_element_type=jnp.float32)
        o_ref[0, :, cols] = (o / l).astype(o_ref.dtype)


def attend(
    dest, q, table, k_arr, v_arr, lo, n_dest, head_dim, first, heads,
    first_block, blocks, key_base, prev=None,
):
    rows, all_width = q.shape
    width = heads * head_dim
    per_dev, block_rows, _ = lo.shape
    tail_blocks = (table.shape[0] - rows) // block_rows
    span = (tail_blocks + 1) * block_rows
    k_rows = k_arr.shape[0]
    kernel = functools.partial(
        attend_kernel,
        heads=heads,
        head_dim=head_dim,
        block_rows=block_rows,
        span=span,
        scale=1.0 / math.sqrt(head_dim),
        first_block=first_block,
        key_base=key_base,
        aliased=prev is not None,
    )
    flops = 4 * blocks * heads * block_rows * span * head_dim
    in_specs = [
        pl.BlockSpec((block_rows, head_dim), functools.partial(
            lambda i, dst, col: (i + first_block, col), col=first + head))
        for head in range(heads)
    ] + [
        pl.BlockSpec((block_rows, head_dim), lambda i, dst: (i + first_block + tail_blocks, 0)),
        pl.BlockSpec((block_rows, head_dim), lambda i, dst: (i + first_block + tail_blocks, 1)),
        pl.BlockSpec((k_rows, head_dim), lambda i, dst: (0, 0)),
        pl.BlockSpec((k_rows, head_dim), lambda i, dst: (0, 0)),
        pl.BlockSpec((1, block_rows, 1), lambda i, dst: (i + first_block, 0, 0)),
    ]
    args = [dest] + [q] * heads + [table, table, k_arr, v_arr, lo]
    aliases = {}
    if prev is not None:
        in_specs.append(pl.BlockSpec(memory_space=pl.ANY))
        args.append(prev)
        aliases = {len(args) - 1: 0}
    grid_spec = pltpu.PrefetchScalarGridSpec(
        num_scalar_prefetch=1,
        grid=(blocks,),
        in_specs=in_specs,
        out_specs=pl.BlockSpec((1, block_rows, width), lambda i, dst: (dst[i + first_block], 0, 0)),
    )
    return pl.pallas_call(
        kernel,
        grid_spec=grid_spec,
        out_shape=jax.ShapeDtypeStruct((n_dest, block_rows, width), q.dtype),
        input_output_aliases=aliases,
        cost_estimate=pl.CostEstimate(
            flops=flops,
            transcendentals=blocks * heads * block_rows * span,
            bytes_accessed=2 * blocks * block_rows * width * 2 + 2 * k_rows * head_dim * 2,
        ),
    )(*args)


def local(queries, keys, values, rope_factors, doc_lengths, owner_map):
    ctx_size = lax.axis_size("ctx")
    ctx_index = lax.axis_index("ctx")
    tp_size = lax.axis_size("tp")
    row_count = queries.shape[0]
    per_dev = owner_map.shape[1]
    block_rows = row_count // per_dev
    tail_rows = row_count // 4
    span = tail_rows + block_rows
    head_dim = 2 * rope_factors.shape[0]
    kv_heads = keys.shape[1] // head_dim
    kv_local = kv_heads // tp_size
    shard_rows = keys.shape[0]

    kv_width = kv_local * head_dim
    kv = jnp.concatenate(
        [
            keys.reshape(shard_rows, tp_size, kv_width).transpose(1, 0, 2),
            values.reshape(shard_rows, tp_size, kv_width).transpose(1, 0, 2),
        ],
        axis=2,
    )
    kv = lax.all_to_all(kv, "tp", split_axis=0, concat_axis=0, tiled=True)
    kv = kv.reshape(row_count, 2 * kv_width)
    k_own_raw = kv[:, :kv_width]
    v_own = kv[:, kv_width:]
    kv_tail = passed_along(kv[row_count - tail_rows :], "ctx", 1)

    ext_rows = row_count + tail_rows
    pos_ext = ctx_index * row_count - tail_rows + jnp.arange(ext_rows, dtype=jnp.int32)
    unused_doc, off_ext = doc_tables(doc_lengths, pos_ext)
    inverse = inverse_freqs(rope_factors, head_dim)
    table = rotation_rows(off_ext, inverse, tail_rows)
    cos_ext = table[:, :head_dim]
    sin_ext = table[:, head_dim:]

    def rotated(raw, cosine, sine):
        raw = raw.astype(jnp.float32)
        return (raw * cosine + jnp.roll(raw, head_dim // 2, axis=1) * sine).astype(jnp.bfloat16)

    k_own = rotated(k_own_raw, cos_ext[tail_rows:], sin_ext[tail_rows:])
    k_tail = rotated(kv_tail[:, :kv_width], cos_ext[:tail_rows], sin_ext[:tail_rows])
    k_ext = jnp.concatenate([k_tail, k_own], axis=0)
    v_ext = jnp.concatenate([kv_tail[:, kv_width:], v_own], axis=0)

    lo = (tail_rows + jnp.arange(row_count, dtype=jnp.int32) % block_rows - off_ext[tail_rows:])
    lo = lo.reshape(per_dev, block_rows, 1)

    devices = jnp.arange(ctx_size, dtype=jnp.int32)
    owner_row = lax.dynamic_index_in_dim(owner_map, ctx_index, 0, keepdims=False)

    q_heads = queries.shape[1] // head_dim
    sizes = [2, 3, 3] if q_heads == 8 else [q_heads]
    tail_blocks = tail_rows // block_rows
    arrived = []
    first = 0
    for number, heads in enumerate(sizes):
        if number == 0:
            send = attend(
                owner_row, queries, table, k_own, v_own, lo, ctx_size, head_dim, first, heads,
                tail_blocks, per_dev - tail_blocks, tail_rows,
            )
            send = attend(
                owner_row, queries, table, k_ext, v_ext, lo, ctx_size, head_dim, first, heads,
                0, tail_blocks, 0, prev=send,
            )
        else:
            send = attend(
                owner_row, queries, table, k_ext, v_ext, lo, ctx_size, head_dim, first, heads,
                0, per_dev, 0,
            )
        arrived.append(lax.all_to_all(send, "ctx", split_axis=0, concat_axis=0, tiled=True))
        first += heads

    sources_match = owner_map == ctx_index
    my_sources = jnp.sum(
        jnp.where(sources_match, devices[:, None], 0), axis=0, dtype=jnp.int32
    )
    finished = jnp.zeros((per_dev, block_rows, queries.shape[1]), queries.dtype)
    first = 0
    for heads, a in zip(sizes, arrived):
        finished = lax.dynamic_update_slice(
            finished, jnp.take(a, my_sources, axis=0, mode="clip"), (0, 0, first * head_dim)
        )
        first += heads
    return finished.reshape(row_count, queries.shape[1])


def solution(mesh):
    in_specs = (P("ctx", "tp"), P(("ctx", "tp"), None), P(("ctx", "tp"), None), P(), P(), P())
    out_specs = P("ctx", "tp")
    return jax.shard_map(local, mesh=mesh, in_specs=in_specs, out_specs=out_specs, check_vma=False)
```

```python
import functools
import math

import jax
import jax.numpy as jnp
from jax import lax
from jax.experimental import pallas as pl
from jax.experimental.pallas import tpu as pltpu
from jax.sharding import PartitionSpec as P

THETA = 500000.0


def passed_along(shard, axis, by):
    length = lax.axis_size(axis)
    pairs = [(i, i + by) for i in range(length) if 0 <= i + by < length]
    return lax.ppermute(shard, axis, pairs)


def doc_tables(lengths, positions):
    doc_ends = jnp.cumsum(lengths, dtype=jnp.int32)
    before = positions[:, None] >= doc_ends[None, :]
    doc_index = jnp.sum(before.astype(jnp.int32), axis=1, dtype=jnp.int32)
    doc_start = jnp.sum(jnp.where(before, lengths[None, :], 0), axis=1, dtype=jnp.int32)
    return (doc_index, positions - doc_start)


def inverse_freqs(factors, head_dim):
    half_dim = head_dim // 2
    exponent = jnp.arange(half_dim, dtype=jnp.float32) * (2.0 / head_dim)
    return 1.0 / (factors * jnp.power(jnp.float32(THETA), exponent))


def rotation_rows(offsets, inverse, distinct):
    angles = jnp.arange(distinct, dtype=jnp.int32).astype(jnp.float32)[:, None] * inverse[None, :]
    cosine = jnp.cos(angles)
    sine = jnp.sin(angles)
    table = jnp.concatenate([cosine, cosine, -sine, sine], axis=1)
    return jnp.take(table, jnp.clip(offsets, 0, distinct - 1), axis=0, mode="clip")


def rotate(vectors, offsets, inverse):
    half_dim = vectors.shape[-1] // 2
    angles = offsets.astype(jnp.float32)[:, None] * inverse[None, :]
    cosine = jnp.cos(angles)
    sine_part = jnp.sin(angles)
    first_half = vectors[..., :half_dim]
    second_half = vectors[..., half_dim:]
    return jnp.concatenate(
        [
            first_half * cosine - second_half * sine_part,
            second_half * cosine + first_half * sine_part,
        ],
        axis=-1,
    )


def attend_kernel(
    dest_ref, *refs, heads, head_dim, block_rows, span, scale, first_block, key_base, aliased
):
    q_refs = refs[:heads]
    cos_ref, sin_ref, k_ref, v_ref, lo_ref = refs[heads : heads + 5]
    o_ref = refs[-1]
    r = pl.program_id(0) + first_block
    start = pl.multiple_of(r * block_rows - key_base, block_rows)
    k = k_ref[pl.ds(start, span), :]
    v = v_ref[pl.ds(start, span), :]
    tail = span - block_rows
    lo = lo_ref[0]
    hi = lax.broadcasted_iota(jnp.int32, (block_rows, 1), 0) + tail
    col = lax.broadcasted_iota(jnp.int32, (block_rows, span), 1)
    visible = (col >= lo) & (col <= hi)
    cos = cos_ref[...]
    sin = sin_ref[...]
    for h in range(heads):
        cols = slice(h * head_dim, (h + 1) * head_dim)
        qh = q_refs[h][...].astype(jnp.float32)
        qr = (qh * cos + pltpu.roll(qh, head_dim // 2, 1) * sin).astype(jnp.bfloat16)
        s = lax.dot_general(
            qr, k, (((1,), (1,)), ((), ())), preferred_element_type=jnp.float32
        ) * scale
        s = jnp.where(visible, s, -1e30)
        m = jnp.max(s, axis=1, keepdims=True)
        p = jnp.exp(s - m)
        l = jnp.sum(p, axis=1, keepdims=True)
        o = jnp.dot(p.astype(jnp.bfloat16), v, preferred_element_type=jnp.float32)
        o_ref[0, :, cols] = (o / l).astype(o_ref.dtype)


def attend(
    dest, q, table, k_arr, v_arr, lo, n_dest, head_dim, first, heads,
    first_block, blocks, key_base, prev=None,
):
    rows, all_width = q.shape
    width = heads * head_dim
    per_dev, block_rows, _ = lo.shape
    tail_blocks = (table.shape[0] - rows) // block_rows
    span = (tail_blocks + 1) * block_rows
    k_rows = k_arr.shape[0]
    kernel = functools.partial(
        attend_kernel,
        heads=heads,
        head_dim=head_dim,
        block_rows=block_rows,
        span=span,
        scale=1.0 / math.sqrt(head_dim),
        first_block=first_block,
        key_base=key_base,
        aliased=prev is not None,
    )
    flops = 4 * blocks * heads * block_rows * span * head_dim
    in_specs = [
        pl.BlockSpec((block_rows, head_dim), functools.partial(
            lambda i, dst, col: (i + first_block, col), col=first + head))
        for head in range(heads)
    ] + [
        pl.BlockSpec((block_rows, head_dim), lambda i, dst: (i + first_block + tail_blocks, 0)),
        pl.BlockSpec((block_rows, head_dim), lambda i, dst: (i + first_block + tail_blocks, 1)),
        pl.BlockSpec((k_rows, head_dim), lambda i, dst: (0, 0)),
        pl.BlockSpec((k_rows, head_dim), lambda i, dst: (0, 0)),
        pl.BlockSpec((1, block_rows, 1), lambda i, dst: (i + first_block, 0, 0)),
    ]
    args = [dest] + [q] * heads + [table, table, k_arr, v_arr, lo]
    aliases = {}
    if prev is not None:
        in_specs.append(pl.BlockSpec(memory_space=pl.ANY))
        args.append(prev)
        aliases = {len(args) - 1: 0}
    grid_spec = pltpu.PrefetchScalarGridSpec(
        num_scalar_prefetch=1,
        grid=(blocks,),
        in_specs=in_specs,
        out_specs=pl.BlockSpec((1, block_rows, width), lambda i, dst: (dst[i + first_block], 0, 0)),
    )
    return pl.pallas_call(
        kernel,
        grid_spec=grid_spec,
        out_shape=jax.ShapeDtypeStruct((n_dest, block_rows, width), q.dtype),
        input_output_aliases=aliases,
        cost_estimate=pl.CostEstimate(
            flops=flops,
            transcendentals=blocks * heads * block_rows * span,
            bytes_accessed=2 * blocks * block_rows * width * 2 + 2 * k_rows * head_dim * 2,
        ),
    )(*args)


def local(queries, keys, values, rope_factors, doc_lengths, owner_map):
    ctx_size = lax.axis_size("ctx")
    ctx_index = lax.axis_index("ctx")
    tp_size = lax.axis_size("tp")
    row_count = queries.shape[0]
    per_dev = owner_map.shape[1]
    block_rows = row_count // per_dev
    tail_rows = row_count // 4
    span = tail_rows + block_rows
    head_dim = 2 * rope_factors.shape[0]
    kv_heads = keys.shape[1] // head_dim
    kv_local = kv_heads // tp_size
    shard_rows = keys.shape[0]

    kv_width = kv_local * head_dim
    kv = jnp.concatenate(
        [
            keys.reshape(shard_rows, tp_size, kv_width).transpose(1, 0, 2),
            values.reshape(shard_rows, tp_size, kv_width).transpose(1, 0, 2),
        ],
        axis=2,
    )
    kv = lax.all_to_all(kv, "tp", split_axis=0, concat_axis=0, tiled=True)
    kv = kv.reshape(row_count, 2 * kv_width)
    k_own_raw = kv[:, :kv_width]
    v_own = kv[:, kv_width:]
    kv_tail = passed_along(kv[row_count - tail_rows :], "ctx", 1)

    ext_rows = row_count + tail_rows
    pos_ext = ctx_index * row_count - tail_rows + jnp.arange(ext_rows, dtype=jnp.int32)
    unused_doc, off_ext = doc_tables(doc_lengths, pos_ext)
    inverse = inverse_freqs(rope_factors, head_dim)
    table = rotation_rows(off_ext, inverse, tail_rows)
    cos_ext = table[:, :head_dim]
    sin_ext = table[:, head_dim:]

    def rotated(raw, cosine, sine):
        raw = raw.astype(jnp.float32)
        return (raw * cosine + jnp.roll(raw, head_dim // 2, axis=1) * sine).astype(jnp.bfloat16)

    k_own = rotated(k_own_raw, cos_ext[tail_rows:], sin_ext[tail_rows:])
    k_tail = rotated(kv_tail[:, :kv_width], cos_ext[:tail_rows], sin_ext[:tail_rows])
    k_ext = jnp.concatenate([k_tail, k_own], axis=0)
    v_ext = jnp.concatenate([kv_tail[:, kv_width:], v_own], axis=0)

    lo = (tail_rows + jnp.arange(row_count, dtype=jnp.int32) % block_rows - off_ext[tail_rows:])
    lo = lo.reshape(per_dev, block_rows, 1)

    devices = jnp.arange(ctx_size, dtype=jnp.int32)
    owner_row = lax.dynamic_index_in_dim(owner_map, ctx_index, 0, keepdims=False)

    q_heads = queries.shape[1] // head_dim
    sizes = [2, 3, 3] if q_heads == 8 else [q_heads]
    tail_blocks = tail_rows // block_rows
    arrived = []
    first = 0
    for number, heads in enumerate(sizes):
        if number == 0:
            send = attend(
                owner_row, queries, table, k_own, v_own, lo, ctx_size, head_dim, first, heads,
                tail_blocks, per_dev - tail_blocks, tail_rows,
            )
            near = tail_rows + tail_rows
            send = attend(
                owner_row, queries, table, k_ext[:near], v_ext[:near], lo, ctx_size, head_dim,
                first, heads, 0, tail_blocks, 0, prev=send,
            )
        else:
            send = attend(
                owner_row, queries, table, k_ext, v_ext, lo, ctx_size, head_dim, first, heads,
                0, per_dev, 0,
            )
        arrived.append(lax.all_to_all(send, "ctx", split_axis=0, concat_axis=0, tiled=True))
        first += heads

    sources_match = owner_map == ctx_index
    my_sources = jnp.sum(
        jnp.where(sources_match, devices[:, None], 0), axis=0, dtype=jnp.int32
    )
    finished = jnp.zeros((per_dev, block_rows, queries.shape[1]), queries.dtype)
    first = 0
    for heads, a in zip(sizes, arrived):
        finished = lax.dynamic_update_slice(
            finished, jnp.take(a, my_sources, axis=0, mode="clip"), (0, 0, first * head_dim)
        )
        first += heads
    return finished.reshape(row_count, queries.shape[1])


def solution(mesh):
    in_specs = (P("ctx", "tp"), P(("ctx", "tp"), None), P(("ctx", "tp"), None), P(), P(), P())
    out_specs = P("ctx", "tp")
    return jax.shard_map(local, mesh=mesh, in_specs=in_specs, out_specs=out_specs, check_vma=False)
```

```python
import functools
import math

import jax
import jax.numpy as jnp
from jax import lax
from jax.experimental import pallas as pl
from jax.experimental.pallas import tpu as pltpu
from jax.sharding import PartitionSpec as P

THETA = 500000.0


def passed_along(shard, axis, by):
    length = lax.axis_size(axis)
    pairs = [(i, i + by) for i in range(length) if 0 <= i + by < length]
    return lax.ppermute(shard, axis, pairs)


def doc_tables(lengths, positions):
    doc_ends = jnp.cumsum(lengths, dtype=jnp.int32)
    before = positions[:, None] >= doc_ends[None, :]
    doc_index = jnp.sum(before.astype(jnp.int32), axis=1, dtype=jnp.int32)
    doc_start = jnp.sum(jnp.where(before, lengths[None, :], 0), axis=1, dtype=jnp.int32)
    return (doc_index, positions - doc_start)


def inverse_freqs(factors, head_dim):
    half_dim = head_dim // 2
    exponent = jnp.arange(half_dim, dtype=jnp.float32) * (2.0 / head_dim)
    return 1.0 / (factors * jnp.power(jnp.float32(THETA), exponent))


def rotation_rows(offsets, inverse, distinct):
    angles = jnp.arange(distinct, dtype=jnp.int32).astype(jnp.float32)[:, None] * inverse[None, :]
    cosine = jnp.cos(angles)
    sine = jnp.sin(angles)
    table = jnp.concatenate([cosine, cosine, -sine, sine], axis=1)
    return jnp.take(table, jnp.clip(offsets, 0, distinct - 1), axis=0, mode="clip")


def rotate(vectors, offsets, inverse):
    half_dim = vectors.shape[-1] // 2
    angles = offsets.astype(jnp.float32)[:, None] * inverse[None, :]
    cosine = jnp.cos(angles)
    sine_part = jnp.sin(angles)
    first_half = vectors[..., :half_dim]
    second_half = vectors[..., half_dim:]
    return jnp.concatenate(
        [
            first_half * cosine - second_half * sine_part,
            second_half * cosine + first_half * sine_part,
        ],
        axis=-1,
    )


def attend_kernel(
    dest_ref, *refs, heads, head_dim, block_rows, span, scale, first_block, key_base, aliased
):
    q_refs = refs[:heads]
    cos_ref, sin_ref, k_ref, v_ref, lo_ref = refs[heads : heads + 5]
    o_ref = refs[-1]
    r = pl.program_id(0) + first_block
    start = pl.multiple_of(r * block_rows - key_base, block_rows)
    k = k_ref[pl.ds(start, span), :]
    v = v_ref[pl.ds(start, span), :]
    tail = span - block_rows
    lo = lo_ref[0]
    hi = lax.broadcasted_iota(jnp.int32, (block_rows, 1), 0) + tail
    col = lax.broadcasted_iota(jnp.int32, (block_rows, span), 1)
    visible = (col >= lo) & (col <= hi)
    cos = cos_ref[...]
    sin = sin_ref[...]
    for h in range(heads):
        cols = slice(h * head_dim, (h + 1) * head_dim)
        qh = q_refs[h][...].astype(jnp.float32)
        qr = (qh * cos + pltpu.roll(qh, head_dim // 2, 1) * sin).astype(jnp.bfloat16)
        s = lax.dot_general(
            qr, k, (((1,), (1,)), ((), ())), preferred_element_type=jnp.float32
        ) * scale
        s = jnp.where(visible, s, -1e30)
        m = jnp.max(s, axis=1, keepdims=True)
        p = jnp.exp(s - m)
        l = jnp.sum(p, axis=1, keepdims=True)
        o = jnp.dot(p.astype(jnp.bfloat16), v, preferred_element_type=jnp.float32)
        o_ref[0, :, cols] = (o / l).astype(o_ref.dtype)


def attend(
    dest, q, table, k_arr, v_arr, lo, n_dest, head_dim, first, heads,
    first_block, blocks, key_base, prev=None, k_col=0, v_col=0,
):
    rows, all_width = q.shape
    width = heads * head_dim
    per_dev, block_rows, _ = lo.shape
    tail_blocks = (table.shape[0] - rows) // block_rows
    span = (tail_blocks + 1) * block_rows
    k_rows = k_arr.shape[0]
    kernel = functools.partial(
        attend_kernel,
        heads=heads,
        head_dim=head_dim,
        block_rows=block_rows,
        span=span,
        scale=1.0 / math.sqrt(head_dim),
        first_block=first_block,
        key_base=key_base,
        aliased=prev is not None,
    )
    flops = 4 * blocks * heads * block_rows * span * head_dim
    in_specs = [
        pl.BlockSpec((block_rows, head_dim), functools.partial(
            lambda i, dst, col: (i + first_block, col), col=first + head))
        for head in range(heads)
    ] + [
        pl.BlockSpec((block_rows, head_dim), lambda i, dst: (i + first_block + tail_blocks, 0)),
        pl.BlockSpec((block_rows, head_dim), lambda i, dst: (i + first_block + tail_blocks, 1)),
        pl.BlockSpec((k_rows, head_dim), lambda i, dst: (0, k_col)),
        pl.BlockSpec((k_rows, head_dim), lambda i, dst: (0, v_col)),
        pl.BlockSpec((1, block_rows, 1), lambda i, dst: (i + first_block, 0, 0)),
    ]
    args = [dest] + [q] * heads + [table, table, k_arr, v_arr, lo]
    aliases = {}
    if prev is not None:
        in_specs.append(pl.BlockSpec(memory_space=pl.ANY))
        args.append(prev)
        aliases = {len(args) - 1: 0}
    grid_spec = pltpu.PrefetchScalarGridSpec(
        num_scalar_prefetch=1,
        grid=(blocks,),
        in_specs=in_specs,
        out_specs=pl.BlockSpec((1, block_rows, width), lambda i, dst: (dst[i + first_block], 0, 0)),
    )
    return pl.pallas_call(
        kernel,
        grid_spec=grid_spec,
        out_shape=jax.ShapeDtypeStruct((n_dest, block_rows, width), q.dtype),
        input_output_aliases=aliases,
        cost_estimate=pl.CostEstimate(
            flops=flops,
            transcendentals=blocks * heads * block_rows * span,
            bytes_accessed=2 * blocks * block_rows * width * 2 + 2 * k_rows * head_dim * 2,
        ),
    )(*args)


def local(queries, keys, values, rope_factors, doc_lengths, owner_map):
    ctx_size = lax.axis_size("ctx")
    ctx_index = lax.axis_index("ctx")
    tp_size = lax.axis_size("tp")
    row_count = queries.shape[0]
    per_dev = owner_map.shape[1]
    block_rows = row_count // per_dev
    tail_rows = row_count // 4
    span = tail_rows + block_rows
    head_dim = 2 * rope_factors.shape[0]
    kv_heads = keys.shape[1] // head_dim
    kv_local = kv_heads // tp_size
    shard_rows = keys.shape[0]

    kv_width = kv_local * head_dim
    kv = jnp.concatenate(
        [
            keys.reshape(shard_rows, tp_size, kv_width).transpose(1, 0, 2),
            values.reshape(shard_rows, tp_size, kv_width).transpose(1, 0, 2),
        ],
        axis=2,
    )
    kv = lax.all_to_all(kv, "tp", split_axis=0, concat_axis=0, tiled=True)
    kv = kv.reshape(row_count, 2 * kv_width)
    k_own_raw = kv[:, :kv_width]
    v_own = kv[:, kv_width:]
    kv_tail = passed_along(kv[row_count - tail_rows :], "ctx", 1)

    ext_rows = row_count + tail_rows
    pos_ext = ctx_index * row_count - tail_rows + jnp.arange(ext_rows, dtype=jnp.int32)
    unused_doc, off_ext = doc_tables(doc_lengths, pos_ext)
    inverse = inverse_freqs(rope_factors, head_dim)
    table = rotation_rows(off_ext, inverse, tail_rows)
    cos_ext = table[:, :head_dim]
    sin_ext = table[:, head_dim:]

    def rotated(raw, cosine, sine):
        raw = raw.astype(jnp.float32)
        return (raw * cosine + jnp.roll(raw, head_dim // 2, axis=1) * sine).astype(jnp.bfloat16)

    k_own = rotated(k_own_raw, cos_ext[tail_rows:], sin_ext[tail_rows:])
    k_tail = rotated(kv_tail[:, :kv_width], cos_ext[:tail_rows], sin_ext[:tail_rows])
    k_ext = jnp.concatenate([k_tail, k_own], axis=0)
    v_ext = jnp.concatenate([kv_tail[:, kv_width:], v_own], axis=0)

    lo = (tail_rows + jnp.arange(row_count, dtype=jnp.int32) % block_rows - off_ext[tail_rows:])
    lo = lo.reshape(per_dev, block_rows, 1)

    devices = jnp.arange(ctx_size, dtype=jnp.int32)
    owner_row = lax.dynamic_index_in_dim(owner_map, ctx_index, 0, keepdims=False)

    q_heads = queries.shape[1] // head_dim
    sizes = [2, 3, 3] if q_heads == 8 else [q_heads]
    tail_blocks = tail_rows // block_rows
    arrived = []
    first = 0
    for number, heads in enumerate(sizes):
        if number == 0:
            send = attend(
                owner_row, queries, table, k_own, v_own, lo, ctx_size, head_dim, first, heads,
                tail_blocks, per_dev - tail_blocks, tail_rows,
            )
            near = jnp.concatenate(
                [
                    jnp.concatenate([k_tail, kv_tail[:, kv_width:]], axis=1),
                    jnp.concatenate([k_own[:tail_rows], v_own[:tail_rows]], axis=1),
                ],
                axis=0,
            )
            send = attend(
                owner_row, queries, table, near, near, lo, ctx_size, head_dim,
                first, heads, 0, tail_blocks, 0, prev=send, k_col=0, v_col=1,
            )
        else:
            send = attend(
                owner_row, queries, table, k_ext, v_ext, lo, ctx_size, head_dim, first, heads,
                0, per_dev, 0,
            )
        arrived.append(lax.all_to_all(send, "ctx", split_axis=0, concat_axis=0, tiled=True))
        first += heads

    sources_match = owner_map == ctx_index
    my_sources = jnp.sum(
        jnp.where(sources_match, devices[:, None], 0), axis=0, dtype=jnp.int32
    )
    finished = jnp.zeros((per_dev, block_rows, queries.shape[1]), queries.dtype)
    first = 0
    for heads, a in zip(sizes, arrived):
        finished = lax.dynamic_update_slice(
            finished, jnp.take(a, my_sources, axis=0, mode="clip"), (0, 0, first * head_dim)
        )
        first += heads
    return finished.reshape(row_count, queries.shape[1])


def solution(mesh):
    in_specs = (P("ctx", "tp"), P(("ctx", "tp"), None), P(("ctx", "tp"), None), P(), P(), P())
    out_specs = P("ctx", "tp")
    return jax.shard_map(local, mesh=mesh, in_specs=in_specs, out_specs=out_specs, check_vma=False)
```

```python
import functools
import math

import jax
import jax.numpy as jnp
from jax import lax
from jax.experimental import pallas as pl
from jax.experimental.pallas import tpu as pltpu
from jax.sharding import PartitionSpec as P

THETA = 500000.0


def passed_along(shard, axis, by):
    length = lax.axis_size(axis)
    pairs = [(i, i + by) for i in range(length) if 0 <= i + by < length]
    return lax.ppermute(shard, axis, pairs)


def doc_tables(lengths, positions):
    doc_ends = jnp.cumsum(lengths, dtype=jnp.int32)
    before = positions[:, None] >= doc_ends[None, :]
    doc_index = jnp.sum(before.astype(jnp.int32), axis=1, dtype=jnp.int32)
    doc_start = jnp.sum(jnp.where(before, lengths[None, :], 0), axis=1, dtype=jnp.int32)
    return (doc_index, positions - doc_start)


def inverse_freqs(factors, head_dim):
    half_dim = head_dim // 2
    exponent = jnp.arange(half_dim, dtype=jnp.float32) * (2.0 / head_dim)
    return 1.0 / (factors * jnp.power(jnp.float32(THETA), exponent))


def rotation_rows(offsets, inverse, distinct):
    angles = jnp.arange(distinct, dtype=jnp.int32).astype(jnp.float32)[:, None] * inverse[None, :]
    cosine = jnp.cos(angles)
    sine = jnp.sin(angles)
    table = jnp.concatenate([cosine, cosine, -sine, sine], axis=1)
    return jnp.take(table, jnp.clip(offsets, 0, distinct - 1), axis=0, mode="clip")


def rotate(vectors, offsets, inverse):
    half_dim = vectors.shape[-1] // 2
    angles = offsets.astype(jnp.float32)[:, None] * inverse[None, :]
    cosine = jnp.cos(angles)
    sine_part = jnp.sin(angles)
    first_half = vectors[..., :half_dim]
    second_half = vectors[..., half_dim:]
    return jnp.concatenate(
        [
            first_half * cosine - second_half * sine_part,
            second_half * cosine + first_half * sine_part,
        ],
        axis=-1,
    )


def attend_kernel(
    dest_ref, kmin_ref, *refs, heads, head_dim, block_rows, span, scale, first_block, key_base,
    aliased,
):
    q_refs = refs[:heads]
    cos_ref, sin_ref, k_ref, v_ref, lo_ref = refs[heads : heads + 5]
    o_ref = refs[-1]
    r = pl.program_id(0) + first_block
    start = pl.multiple_of(r * block_rows - key_base, block_rows)
    tail = span - block_rows
    lo = lo_ref[0]
    hi = lax.broadcasted_iota(jnp.int32, (block_rows, 1), 0) + tail
    cos = cos_ref[...]
    sin = sin_ref[...]

    def window(skip):
        width = span - skip
        k = k_ref[pl.ds(start + skip, width), :]
        v = v_ref[pl.ds(start + skip, width), :]
        col = lax.broadcasted_iota(jnp.int32, (block_rows, width), 1) + skip
        visible = (col >= lo) & (col <= hi)
        for h in range(heads):
            cols = slice(h * head_dim, (h + 1) * head_dim)
            qh = q_refs[h][...].astype(jnp.float32)
            qr = (qh * cos + pltpu.roll(qh, head_dim // 2, 1) * sin).astype(jnp.bfloat16)
            s = lax.dot_general(
                qr, k, (((1,), (1,)), ((), ())), preferred_element_type=jnp.float32
            ) * scale
            s = jnp.where(visible, s, -1e30)
            m = jnp.max(s, axis=1, keepdims=True)
            p = jnp.exp(s - m)
            l = jnp.sum(p, axis=1, keepdims=True)
            o = jnp.dot(p.astype(jnp.bfloat16), v, preferred_element_type=jnp.float32)
            o_ref[0, :, cols] = (o / l).astype(o_ref.dtype)

    kmin = kmin_ref[r]

    @pl.when(kmin >= block_rows)
    def _():
        window(block_rows)

    @pl.when(kmin < block_rows)
    def _():
        window(0)


def attend(
    dest, kmin, q, table, k_arr, v_arr, lo, n_dest, head_dim, first, heads,
    first_block, blocks, key_base, prev=None, k_col=0, v_col=0,
):
    rows, all_width = q.shape
    width = heads * head_dim
    per_dev, block_rows, _ = lo.shape
    tail_blocks = (table.shape[0] - rows) // block_rows
    span = (tail_blocks + 1) * block_rows
    k_rows = k_arr.shape[0]
    kernel = functools.partial(
        attend_kernel,
        heads=heads,
        head_dim=head_dim,
        block_rows=block_rows,
        span=span,
        scale=1.0 / math.sqrt(head_dim),
        first_block=first_block,
        key_base=key_base,
        aliased=prev is not None,
    )
    flops = 4 * blocks * heads * block_rows * span * head_dim
    in_specs = [
        pl.BlockSpec((block_rows, head_dim), functools.partial(
            lambda i, dst, km, col: (i + first_block, col), col=first + head))
        for head in range(heads)
    ] + [
        pl.BlockSpec((block_rows, head_dim), lambda i, dst, km: (i + first_block + tail_blocks, 0)),
        pl.BlockSpec((block_rows, head_dim), lambda i, dst, km: (i + first_block + tail_blocks, 1)),
        pl.BlockSpec((k_rows, head_dim), lambda i, dst, km: (0, k_col)),
        pl.BlockSpec((k_rows, head_dim), lambda i, dst, km: (0, v_col)),
        pl.BlockSpec((1, block_rows, 1), lambda i, dst, km: (i + first_block, 0, 0)),
    ]
    args = [dest, kmin] + [q] * heads + [table, table, k_arr, v_arr, lo]
    aliases = {}
    if prev is not None:
        in_specs.append(pl.BlockSpec(memory_space=pl.ANY))
        args.append(prev)
        aliases = {len(args) - 1: 0}
    grid_spec = pltpu.PrefetchScalarGridSpec(
        num_scalar_prefetch=2,
        grid=(blocks,),
        in_specs=in_specs,
        out_specs=pl.BlockSpec(
            (1, block_rows, width), lambda i, dst, km: (dst[i + first_block], 0, 0)
        ),
    )
    return pl.pallas_call(
        kernel,
        grid_spec=grid_spec,
        out_shape=jax.ShapeDtypeStruct((n_dest, block_rows, width), q.dtype),
        input_output_aliases=aliases,
        cost_estimate=pl.CostEstimate(
            flops=flops,
            transcendentals=blocks * heads * block_rows * span,
            bytes_accessed=2 * blocks * block_rows * width * 2 + 2 * k_rows * head_dim * 2,
        ),
    )(*args)


def local(queries, keys, values, rope_factors, doc_lengths, owner_map):
    ctx_size = lax.axis_size("ctx")
    ctx_index = lax.axis_index("ctx")
    tp_size = lax.axis_size("tp")
    row_count = queries.shape[0]
    per_dev = owner_map.shape[1]
    block_rows = row_count // per_dev
    tail_rows = row_count // 4
    span = tail_rows + block_rows
    head_dim = 2 * rope_factors.shape[0]
    kv_heads = keys.shape[1] // head_dim
    kv_local = kv_heads // tp_size
    shard_rows = keys.shape[0]

    kv_width = kv_local * head_dim
    kv = jnp.concatenate(
        [
            keys.reshape(shard_rows, tp_size, kv_width).transpose(1, 0, 2),
            values.reshape(shard_rows, tp_size, kv_width).transpose(1, 0, 2),
        ],
        axis=2,
    )
    kv = lax.all_to_all(kv, "tp", split_axis=0, concat_axis=0, tiled=True)
    kv = kv.reshape(row_count, 2 * kv_width)
    k_own_raw = kv[:, :kv_width]
    v_own = kv[:, kv_width:]
    kv_tail = passed_along(kv[row_count - tail_rows :], "ctx", 1)

    ext_rows = row_count + tail_rows
    pos_ext = ctx_index * row_count - tail_rows + jnp.arange(ext_rows, dtype=jnp.int32)
    unused_doc, off_ext = doc_tables(doc_lengths, pos_ext)
    inverse = inverse_freqs(rope_factors, head_dim)
    table = rotation_rows(off_ext, inverse, tail_rows)
    cos_ext = table[:, :head_dim]
    sin_ext = table[:, head_dim:]

    def rotated(raw, cosine, sine):
        raw = raw.astype(jnp.float32)
        return (raw * cosine + jnp.roll(raw, head_dim // 2, axis=1) * sine).astype(jnp.bfloat16)

    k_own = rotated(k_own_raw, cos_ext[tail_rows:], sin_ext[tail_rows:])
    k_tail = rotated(kv_tail[:, :kv_width], cos_ext[:tail_rows], sin_ext[:tail_rows])
    k_ext = jnp.concatenate([k_tail, k_own], axis=0)
    v_ext = jnp.concatenate([kv_tail[:, kv_width:], v_own], axis=0)

    lo = (tail_rows + jnp.arange(row_count, dtype=jnp.int32) % block_rows - off_ext[tail_rows:])
    lo = lo.reshape(per_dev, block_rows, 1)
    kmin = lo[:, 0, 0]

    devices = jnp.arange(ctx_size, dtype=jnp.int32)
    owner_row = lax.dynamic_index_in_dim(owner_map, ctx_index, 0, keepdims=False)

    q_heads = queries.shape[1] // head_dim
    sizes = [2, 3, 3] if q_heads == 8 else [q_heads]
    tail_blocks = tail_rows // block_rows
    arrived = []
    first = 0
    for number, heads in enumerate(sizes):
        if number == 0:
            send = attend(
                owner_row, kmin, queries, table, k_own, v_own, lo, ctx_size, head_dim, first, heads,
                tail_blocks, per_dev - tail_blocks, tail_rows,
            )
            near = jnp.concatenate(
                [
                    jnp.concatenate([k_tail, kv_tail[:, kv_width:]], axis=1),
                    jnp.concatenate([k_own[:tail_rows], v_own[:tail_rows]], axis=1),
                ],
                axis=0,
            )
            send = attend(
                owner_row, kmin, queries, table, near, near, lo, ctx_size, head_dim,
                first, heads, 0, tail_blocks, 0, prev=send, k_col=0, v_col=1,
            )
        else:
            send = attend(
                owner_row, kmin, queries, table, k_ext, v_ext, lo, ctx_size, head_dim, first, heads,
                0, per_dev, 0,
            )
        arrived.append(lax.all_to_all(send, "ctx", split_axis=0, concat_axis=0, tiled=True))
        first += heads

    sources_match = owner_map == ctx_index
    my_sources = jnp.sum(
        jnp.where(sources_match, devices[:, None], 0), axis=0, dtype=jnp.int32
    )
    finished = jnp.zeros((per_dev, block_rows, queries.shape[1]), queries.dtype)
    first = 0
    for heads, a in zip(sizes, arrived):
        finished = lax.dynamic_update_slice(
            finished, jnp.take(a, my_sources, axis=0, mode="clip"), (0, 0, first * head_dim)
        )
        first += heads
    return finished.reshape(row_count, queries.shape[1])


def solution(mesh):
    in_specs = (P("ctx", "tp"), P(("ctx", "tp"), None), P(("ctx", "tp"), None), P(), P(), P())
    out_specs = P("ctx", "tp")
    return jax.shard_map(local, mesh=mesh, in_specs=in_specs, out_specs=out_specs, check_vma=False)
```

```python
import functools
import math

import jax
import jax.numpy as jnp
from jax import lax
from jax.experimental import pallas as pl
from jax.experimental.pallas import tpu as pltpu
from jax.sharding import PartitionSpec as P

THETA = 500000.0


def passed_along(shard, axis, by):
    length = lax.axis_size(axis)
    pairs = [(i, i + by) for i in range(length) if 0 <= i + by < length]
    return lax.ppermute(shard, axis, pairs)


def doc_tables(lengths, positions):
    doc_ends = jnp.cumsum(lengths, dtype=jnp.int32)
    before = positions[:, None] >= doc_ends[None, :]
    doc_index = jnp.sum(before.astype(jnp.int32), axis=1, dtype=jnp.int32)
    doc_start = jnp.sum(jnp.where(before, lengths[None, :], 0), axis=1, dtype=jnp.int32)
    return (doc_index, positions - doc_start)


def inverse_freqs(factors, head_dim):
    half_dim = head_dim // 2
    exponent = jnp.arange(half_dim, dtype=jnp.float32) * (2.0 / head_dim)
    return 1.0 / (factors * jnp.power(jnp.float32(THETA), exponent))


def rotation_rows(offsets, inverse, distinct):
    angles = jnp.arange(distinct, dtype=jnp.int32).astype(jnp.float32)[:, None] * inverse[None, :]
    cosine = jnp.cos(angles)
    sine = jnp.sin(angles)
    table = jnp.concatenate([cosine, cosine, -sine, sine], axis=1)
    return jnp.take(table, jnp.clip(offsets, 0, distinct - 1), axis=0, mode="clip")


def rotate(vectors, offsets, inverse):
    half_dim = vectors.shape[-1] // 2
    angles = offsets.astype(jnp.float32)[:, None] * inverse[None, :]
    cosine = jnp.cos(angles)
    sine_part = jnp.sin(angles)
    first_half = vectors[..., :half_dim]
    second_half = vectors[..., half_dim:]
    return jnp.concatenate(
        [
            first_half * cosine - second_half * sine_part,
            second_half * cosine + first_half * sine_part,
        ],
        axis=-1,
    )


def attend_kernel(
    dest_ref, kmin_ref, *refs, heads, head_dim, block_rows, span, scale, first_block, key_base,
    aliased,
):
    q_refs = refs[:heads]
    cos_ref, sin_ref, k_ref, v_ref, lo_ref = refs[heads : heads + 5]
    o_ref = refs[-1]
    r = pl.program_id(0) + first_block
    start = pl.multiple_of(r * block_rows - key_base, block_rows)
    tail = span - block_rows
    lo = lo_ref[0]
    hi = lax.broadcasted_iota(jnp.int32, (block_rows, 1), 0) + tail
    cos = cos_ref[...]
    sin = sin_ref[...]

    def window(skip):
        width = span - skip
        first_key = pl.multiple_of(start + skip, 128)
        k = k_ref[pl.ds(first_key, width), :]
        v = v_ref[pl.ds(first_key, width), :]
        col = lax.broadcasted_iota(jnp.int32, (block_rows, width), 1) + skip
        visible = (col >= lo) & (col <= hi)
        for h in range(heads):
            cols = slice(h * head_dim, (h + 1) * head_dim)
            qh = q_refs[h][...].astype(jnp.float32)
            qr = (qh * cos + pltpu.roll(qh, head_dim // 2, 1) * sin).astype(jnp.bfloat16)
            s = lax.dot_general(
                qr, k, (((1,), (1,)), ((), ())), preferred_element_type=jnp.float32
            ) * scale
            s = jnp.where(visible, s, -1e30)
            m = jnp.max(s, axis=1, keepdims=True)
            p = jnp.exp(s - m)
            l = jnp.sum(p, axis=1, keepdims=True)
            o = jnp.dot(p.astype(jnp.bfloat16), v, preferred_element_type=jnp.float32)
            o_ref[0, :, cols] = (o / l).astype(o_ref.dtype)

    tile = 128
    tiles = lax.min(kmin_ref[r] // tile, (span - block_rows) // tile - 1)
    for skipped in range((span - block_rows) // tile):

        @pl.when(tiles == skipped)
        def _():
            window(skipped * tile)


def attend(
    dest, kmin, q, table, k_arr, v_arr, lo, n_dest, head_dim, first, heads,
    first_block, blocks, key_base, prev=None, k_col=0, v_col=0,
):
    rows, all_width = q.shape
    width = heads * head_dim
    per_dev, block_rows, _ = lo.shape
    tail_blocks = (table.shape[0] - rows) // block_rows
    span = (tail_blocks + 1) * block_rows
    k_rows = k_arr.shape[0]
    kernel = functools.partial(
        attend_kernel,
        heads=heads,
        head_dim=head_dim,
        block_rows=block_rows,
        span=span,
        scale=1.0 / math.sqrt(head_dim),
        first_block=first_block,
        key_base=key_base,
        aliased=prev is not None,
    )
    flops = 4 * blocks * heads * block_rows * span * head_dim
    in_specs = [
        pl.BlockSpec((block_rows, head_dim), functools.partial(
            lambda i, dst, km, col: (i + first_block, col), col=first + head))
        for head in range(heads)
    ] + [
        pl.BlockSpec((block_rows, head_dim), lambda i, dst, km: (i + first_block + tail_blocks, 0)),
        pl.BlockSpec((block_rows, head_dim), lambda i, dst, km: (i + first_block + tail_blocks, 1)),
        pl.BlockSpec((k_rows, head_dim), lambda i, dst, km: (0, k_col)),
        pl.BlockSpec((k_rows, head_dim), lambda i, dst, km: (0, v_col)),
        pl.BlockSpec((1, block_rows, 1), lambda i, dst, km: (i + first_block, 0, 0)),
    ]
    args = [dest, kmin] + [q] * heads + [table, table, k_arr, v_arr, lo]
    aliases = {}
    if prev is not None:
        in_specs.append(pl.BlockSpec(memory_space=pl.ANY))
        args.append(prev)
        aliases = {len(args) - 1: 0}
    grid_spec = pltpu.PrefetchScalarGridSpec(
        num_scalar_prefetch=2,
        grid=(blocks,),
        in_specs=in_specs,
        out_specs=pl.BlockSpec(
            (1, block_rows, width), lambda i, dst, km: (dst[i + first_block], 0, 0)
        ),
    )
    return pl.pallas_call(
        kernel,
        grid_spec=grid_spec,
        out_shape=jax.ShapeDtypeStruct((n_dest, block_rows, width), q.dtype),
        input_output_aliases=aliases,
        cost_estimate=pl.CostEstimate(
            flops=flops,
            transcendentals=blocks * heads * block_rows * span,
            bytes_accessed=2 * blocks * block_rows * width * 2 + 2 * k_rows * head_dim * 2,
        ),
    )(*args)


def local(queries, keys, values, rope_factors, doc_lengths, owner_map):
    ctx_size = lax.axis_size("ctx")
    ctx_index = lax.axis_index("ctx")
    tp_size = lax.axis_size("tp")
    row_count = queries.shape[0]
    per_dev = owner_map.shape[1]
    block_rows = row_count // per_dev
    tail_rows = row_count // 4
    span = tail_rows + block_rows
    head_dim = 2 * rope_factors.shape[0]
    kv_heads = keys.shape[1] // head_dim
    kv_local = kv_heads // tp_size
    shard_rows = keys.shape[0]

    kv_width = kv_local * head_dim
    kv = jnp.concatenate(
        [
            keys.reshape(shard_rows, tp_size, kv_width).transpose(1, 0, 2),
            values.reshape(shard_rows, tp_size, kv_width).transpose(1, 0, 2),
        ],
        axis=2,
    )
    kv = lax.all_to_all(kv, "tp", split_axis=0, concat_axis=0, tiled=True)
    kv = kv.reshape(row_count, 2 * kv_width)
    k_own_raw = kv[:, :kv_width]
    v_own = kv[:, kv_width:]
    kv_tail = passed_along(kv[row_count - tail_rows :], "ctx", 1)

    ext_rows = row_count + tail_rows
    pos_ext = ctx_index * row_count - tail_rows + jnp.arange(ext_rows, dtype=jnp.int32)
    unused_doc, off_ext = doc_tables(doc_lengths, pos_ext)
    inverse = inverse_freqs(rope_factors, head_dim)
    table = rotation_rows(off_ext, inverse, tail_rows)
    cos_ext = table[:, :head_dim]
    sin_ext = table[:, head_dim:]

    def rotated(raw, cosine, sine):
        raw = raw.astype(jnp.float32)
        return (raw * cosine + jnp.roll(raw, head_dim // 2, axis=1) * sine).astype(jnp.bfloat16)

    k_own = rotated(k_own_raw, cos_ext[tail_rows:], sin_ext[tail_rows:])
    k_tail = rotated(kv_tail[:, :kv_width], cos_ext[:tail_rows], sin_ext[:tail_rows])
    k_ext = jnp.concatenate([k_tail, k_own], axis=0)
    v_ext = jnp.concatenate([kv_tail[:, kv_width:], v_own], axis=0)

    lo = (tail_rows + jnp.arange(row_count, dtype=jnp.int32) % block_rows - off_ext[tail_rows:])
    lo = lo.reshape(per_dev, block_rows, 1)
    kmin = lo[:, 0, 0]

    devices = jnp.arange(ctx_size, dtype=jnp.int32)
    owner_row = lax.dynamic_index_in_dim(owner_map, ctx_index, 0, keepdims=False)

    q_heads = queries.shape[1] // head_dim
    sizes = [2, 3, 3] if q_heads == 8 else [q_heads]
    tail_blocks = tail_rows // block_rows
    arrived = []
    first = 0
    for number, heads in enumerate(sizes):
        if number == 0:
            send = attend(
                owner_row, kmin, queries, table, k_own, v_own, lo, ctx_size, head_dim, first, heads,
                tail_blocks, per_dev - tail_blocks, tail_rows,
            )
            near = jnp.concatenate(
                [
                    jnp.concatenate([k_tail, kv_tail[:, kv_width:]], axis=1),
                    jnp.concatenate([k_own[:tail_rows], v_own[:tail_rows]], axis=1),
                ],
                axis=0,
            )
            send = attend(
                owner_row, kmin, queries, table, near, near, lo, ctx_size, head_dim,
                first, heads, 0, tail_blocks, 0, prev=send, k_col=0, v_col=1,
            )
        else:
            send = attend(
                owner_row, kmin, queries, table, k_ext, v_ext, lo, ctx_size, head_dim, first, heads,
                0, per_dev, 0,
            )
        arrived.append(lax.all_to_all(send, "ctx", split_axis=0, concat_axis=0, tiled=True))
        first += heads

    sources_match = owner_map == ctx_index
    my_sources = jnp.sum(
        jnp.where(sources_match, devices[:, None], 0), axis=0, dtype=jnp.int32
    )
    finished = jnp.zeros((per_dev, block_rows, queries.shape[1]), queries.dtype)
    first = 0
    for heads, a in zip(sizes, arrived):
        finished = lax.dynamic_update_slice(
            finished, jnp.take(a, my_sources, axis=0, mode="clip"), (0, 0, first * head_dim)
        )
        first += heads
    return finished.reshape(row_count, queries.shape[1])


def solution(mesh):
    in_specs = (P("ctx", "tp"), P(("ctx", "tp"), None), P(("ctx", "tp"), None), P(), P(), P())
    out_specs = P("ctx", "tp")
    return jax.shard_map(local, mesh=mesh, in_specs=in_specs, out_specs=out_specs, check_vma=False)
```

```python
import functools
import math

import jax
import jax.numpy as jnp
from jax import lax
from jax.experimental import pallas as pl
from jax.experimental.pallas import tpu as pltpu
from jax.sharding import PartitionSpec as P

THETA = 500000.0


def passed_along(shard, axis, by):
    length = lax.axis_size(axis)
    pairs = [(i, i + by) for i in range(length) if 0 <= i + by < length]
    return lax.ppermute(shard, axis, pairs)


def doc_tables(lengths, positions):
    doc_ends = jnp.cumsum(lengths, dtype=jnp.int32)
    before = positions[:, None] >= doc_ends[None, :]
    doc_index = jnp.sum(before.astype(jnp.int32), axis=1, dtype=jnp.int32)
    doc_start = jnp.sum(jnp.where(before, lengths[None, :], 0), axis=1, dtype=jnp.int32)
    return (doc_index, positions - doc_start)


def inverse_freqs(factors, head_dim):
    half_dim = head_dim // 2
    exponent = jnp.arange(half_dim, dtype=jnp.float32) * (2.0 / head_dim)
    return 1.0 / (factors * jnp.power(jnp.float32(THETA), exponent))


def rotation_rows(offsets, inverse, distinct):
    angles = jnp.arange(distinct, dtype=jnp.int32).astype(jnp.float32)[:, None] * inverse[None, :]
    cosine = jnp.cos(angles)
    sine = jnp.sin(angles)
    table = jnp.concatenate([cosine, cosine, -sine, sine], axis=1)
    return jnp.take(table, jnp.clip(offsets, 0, distinct - 1), axis=0, mode="clip")


def rotate(vectors, offsets, inverse):
    half_dim = vectors.shape[-1] // 2
    angles = offsets.astype(jnp.float32)[:, None] * inverse[None, :]
    cosine = jnp.cos(angles)
    sine_part = jnp.sin(angles)
    first_half = vectors[..., :half_dim]
    second_half = vectors[..., half_dim:]
    return jnp.concatenate(
        [
            first_half * cosine - second_half * sine_part,
            second_half * cosine + first_half * sine_part,
        ],
        axis=-1,
    )


def attend_kernel(
    dest_ref, kmin_ref, *refs, heads, head_dim, block_rows, span, scale, first_block, key_base,
    aliased,
):
    q_refs = refs[:heads]
    parts = span // block_rows
    cos_ref, sin_ref = refs[heads : heads + 2]
    k_refs = refs[heads + 2 : heads + 2 + parts]
    v_refs = refs[heads + 2 + parts : heads + 2 + 2 * parts]
    lo_ref = refs[heads + 2 + 2 * parts]
    o_ref = refs[-1]
    r = pl.program_id(0) + first_block
    tail = span - block_rows
    lo = lo_ref[0]
    hi = lax.broadcasted_iota(jnp.int32, (block_rows, 1), 0) + tail
    cos = cos_ref[...]
    sin = sin_ref[...]

    def window(skip):
        width = span - skip
        used = range(skip // block_rows, parts)
        k = jnp.concatenate([k_refs[w][...] for w in used], axis=0)
        v = jnp.concatenate([v_refs[w][...] for w in used], axis=0)
        col = lax.broadcasted_iota(jnp.int32, (block_rows, width), 1) + skip
        visible = (col >= lo) & (col <= hi)
        for h in range(heads):
            cols = slice(h * head_dim, (h + 1) * head_dim)
            qh = q_refs[h][...].astype(jnp.float32)
            qr = (qh * cos + pltpu.roll(qh, head_dim // 2, 1) * sin).astype(jnp.bfloat16)
            s = lax.dot_general(
                qr, k, (((1,), (1,)), ((), ())), preferred_element_type=jnp.float32
            ) * scale
            s = jnp.where(visible, s, -1e30)
            m = jnp.max(s, axis=1, keepdims=True)
            p = jnp.exp(s - m)
            l = jnp.sum(p, axis=1, keepdims=True)
            o = jnp.dot(p.astype(jnp.bfloat16), v, preferred_element_type=jnp.float32)
            o_ref[0, :, cols] = (o / l).astype(o_ref.dtype)

    kmin = kmin_ref[r]

    @pl.when(kmin >= block_rows)
    def _():
        window(block_rows)

    @pl.when(kmin < block_rows)
    def _():
        window(0)


def attend(
    dest, kmin, q, table, k_arr, v_arr, lo, n_dest, head_dim, first, heads,
    first_block, blocks, key_base, prev=None, k_col=0, v_col=0,
):
    rows, all_width = q.shape
    width = heads * head_dim
    per_dev, block_rows, _ = lo.shape
    tail_blocks = (table.shape[0] - rows) // block_rows
    span = (tail_blocks + 1) * block_rows
    k_rows = k_arr.shape[0]
    kernel = functools.partial(
        attend_kernel,
        heads=heads,
        head_dim=head_dim,
        block_rows=block_rows,
        span=span,
        scale=1.0 / math.sqrt(head_dim),
        first_block=first_block,
        key_base=key_base,
        aliased=prev is not None,
    )
    flops = 4 * blocks * heads * block_rows * span * head_dim
    in_specs = [
        pl.BlockSpec((block_rows, head_dim), functools.partial(
            lambda i, dst, km, col: (i + first_block, col), col=first + head))
        for head in range(heads)
    ] + [
        pl.BlockSpec((block_rows, head_dim), lambda i, dst, km: (i + first_block + tail_blocks, 0)),
        pl.BlockSpec((block_rows, head_dim), lambda i, dst, km: (i + first_block + tail_blocks, 1)),
    ] + [
        pl.BlockSpec((block_rows, head_dim), functools.partial(
            lambda i, dst, km, w, c: (i + first_block - key_base // block_rows + w, c), w=w, c=c))
        for c in (k_col, v_col) for w in range(tail_blocks + 1)
    ] + [
        pl.BlockSpec((1, block_rows, 1), lambda i, dst, km: (i + first_block, 0, 0)),
    ]
    parts = tail_blocks + 1
    args = [dest, kmin] + [q] * heads + [table, table] + [k_arr] * parts + [v_arr] * parts + [lo]
    aliases = {}
    if prev is not None:
        in_specs.append(pl.BlockSpec(memory_space=pl.ANY))
        args.append(prev)
        aliases = {len(args) - 1: 0}
    grid_spec = pltpu.PrefetchScalarGridSpec(
        num_scalar_prefetch=2,
        grid=(blocks,),
        in_specs=in_specs,
        out_specs=pl.BlockSpec(
            (1, block_rows, width), lambda i, dst, km: (dst[i + first_block], 0, 0)
        ),
    )
    return pl.pallas_call(
        kernel,
        grid_spec=grid_spec,
        out_shape=jax.ShapeDtypeStruct((n_dest, block_rows, width), q.dtype),
        input_output_aliases=aliases,
        cost_estimate=pl.CostEstimate(
            flops=flops,
            transcendentals=blocks * heads * block_rows * span,
            bytes_accessed=2 * blocks * block_rows * width * 2 + 2 * k_rows * head_dim * 2,
        ),
    )(*args)


def local(queries, keys, values, rope_factors, doc_lengths, owner_map):
    ctx_size = lax.axis_size("ctx")
    ctx_index = lax.axis_index("ctx")
    tp_size = lax.axis_size("tp")
    row_count = queries.shape[0]
    per_dev = owner_map.shape[1]
    block_rows = row_count // per_dev
    tail_rows = row_count // 4
    span = tail_rows + block_rows
    head_dim = 2 * rope_factors.shape[0]
    kv_heads = keys.shape[1] // head_dim
    kv_local = kv_heads // tp_size
    shard_rows = keys.shape[0]

    kv_width = kv_local * head_dim
    kv = jnp.concatenate(
        [
            keys.reshape(shard_rows, tp_size, kv_width).transpose(1, 0, 2),
            values.reshape(shard_rows, tp_size, kv_width).transpose(1, 0, 2),
        ],
        axis=2,
    )
    kv = lax.all_to_all(kv, "tp", split_axis=0, concat_axis=0, tiled=True)
    kv = kv.reshape(row_count, 2 * kv_width)
    k_own_raw = kv[:, :kv_width]
    v_own = kv[:, kv_width:]
    kv_tail = passed_along(kv[row_count - tail_rows :], "ctx", 1)

    ext_rows = row_count + tail_rows
    pos_ext = ctx_index * row_count - tail_rows + jnp.arange(ext_rows, dtype=jnp.int32)
    unused_doc, off_ext = doc_tables(doc_lengths, pos_ext)
    inverse = inverse_freqs(rope_factors, head_dim)
    table = rotation_rows(off_ext, inverse, tail_rows)
    cos_ext = table[:, :head_dim]
    sin_ext = table[:, head_dim:]

    def rotated(raw, cosine, sine):
        raw = raw.astype(jnp.float32)
        return (raw * cosine + jnp.roll(raw, head_dim // 2, axis=1) * sine).astype(jnp.bfloat16)

    k_own = rotated(k_own_raw, cos_ext[tail_rows:], sin_ext[tail_rows:])
    k_tail = rotated(kv_tail[:, :kv_width], cos_ext[:tail_rows], sin_ext[:tail_rows])
    k_ext = jnp.concatenate([k_tail, k_own], axis=0)
    v_ext = jnp.concatenate([kv_tail[:, kv_width:], v_own], axis=0)

    lo = (tail_rows + jnp.arange(row_count, dtype=jnp.int32) % block_rows - off_ext[tail_rows:])
    lo = lo.reshape(per_dev, block_rows, 1)
    kmin = lo[:, 0, 0]

    devices = jnp.arange(ctx_size, dtype=jnp.int32)
    owner_row = lax.dynamic_index_in_dim(owner_map, ctx_index, 0, keepdims=False)

    q_heads = queries.shape[1] // head_dim
    sizes = [2, 3, 3] if q_heads == 8 else [q_heads]
    tail_blocks = tail_rows // block_rows
    arrived = []
    first = 0
    for number, heads in enumerate(sizes):
        if number == 0:
            send = attend(
                owner_row, kmin, queries, table, k_own, v_own, lo, ctx_size, head_dim, first, heads,
                tail_blocks, per_dev - tail_blocks, tail_rows,
            )
            near = jnp.concatenate(
                [
                    jnp.concatenate([k_tail, kv_tail[:, kv_width:]], axis=1),
                    jnp.concatenate([k_own[:tail_rows], v_own[:tail_rows]], axis=1),
                ],
                axis=0,
            )
            send = attend(
                owner_row, kmin, queries, table, near, near, lo, ctx_size, head_dim,
                first, heads, 0, tail_blocks, 0, prev=send, k_col=0, v_col=1,
            )
        else:
            send = attend(
                owner_row, kmin, queries, table, k_ext, v_ext, lo, ctx_size, head_dim, first, heads,
                0, per_dev, 0,
            )
        arrived.append(lax.all_to_all(send, "ctx", split_axis=0, concat_axis=0, tiled=True))
        first += heads

    sources_match = owner_map == ctx_index
    my_sources = jnp.sum(
        jnp.where(sources_match, devices[:, None], 0), axis=0, dtype=jnp.int32
    )
    finished = jnp.zeros((per_dev, block_rows, queries.shape[1]), queries.dtype)
    first = 0
    for heads, a in zip(sizes, arrived):
        finished = lax.dynamic_update_slice(
            finished, jnp.take(a, my_sources, axis=0, mode="clip"), (0, 0, first * head_dim)
        )
        first += heads
    return finished.reshape(row_count, queries.shape[1])


def solution(mesh):
    in_specs = (P("ctx", "tp"), P(("ctx", "tp"), None), P(("ctx", "tp"), None), P(), P(), P())
    out_specs = P("ctx", "tp")
    return jax.shard_map(local, mesh=mesh, in_specs=in_specs, out_specs=out_specs, check_vma=False)
```

```python
import functools
import math

import jax
import jax.numpy as jnp
from jax import lax
from jax.experimental import pallas as pl
from jax.experimental.pallas import tpu as pltpu
from jax.sharding import PartitionSpec as P

THETA = 500000.0


def passed_along(shard, axis, by):
    length = lax.axis_size(axis)
    pairs = [(i, i + by) for i in range(length) if 0 <= i + by < length]
    return lax.ppermute(shard, axis, pairs)


def doc_tables(lengths, positions):
    doc_ends = jnp.cumsum(lengths, dtype=jnp.int32)
    before = positions[:, None] >= doc_ends[None, :]
    doc_index = jnp.sum(before.astype(jnp.int32), axis=1, dtype=jnp.int32)
    doc_start = jnp.sum(jnp.where(before, lengths[None, :], 0), axis=1, dtype=jnp.int32)
    return (doc_index, positions - doc_start)


def inverse_freqs(factors, head_dim):
    half_dim = head_dim // 2
    exponent = jnp.arange(half_dim, dtype=jnp.float32) * (2.0 / head_dim)
    return 1.0 / (factors * jnp.power(jnp.float32(THETA), exponent))


def rotation_rows(offsets, inverse, distinct):
    angles = jnp.arange(distinct, dtype=jnp.int32).astype(jnp.float32)[:, None] * inverse[None, :]
    cosine = jnp.cos(angles)
    sine = jnp.sin(angles)
    table = jnp.concatenate([cosine, cosine, -sine, sine], axis=1)
    return jnp.take(table, jnp.clip(offsets, 0, distinct - 1), axis=0, mode="clip")


def rotate(vectors, offsets, inverse):
    half_dim = vectors.shape[-1] // 2
    angles = offsets.astype(jnp.float32)[:, None] * inverse[None, :]
    cosine = jnp.cos(angles)
    sine_part = jnp.sin(angles)
    first_half = vectors[..., :half_dim]
    second_half = vectors[..., half_dim:]
    return jnp.concatenate(
        [
            first_half * cosine - second_half * sine_part,
            second_half * cosine + first_half * sine_part,
        ],
        axis=-1,
    )


def attend_kernel(
    dest_ref, kmin_ref, *refs, heads, head_dim, block_rows, span, scale, first_block, key_base,
    aliased,
):
    q_refs = refs[:heads]
    cos_ref, sin_ref, k_ref, v_ref, lo_ref = refs[heads : heads + 5]
    o_ref = refs[-1]
    r = pl.program_id(0) + first_block
    start = pl.multiple_of(r * block_rows - key_base, block_rows)
    tail = span - block_rows
    lo = lo_ref[0]
    hi = lax.broadcasted_iota(jnp.int32, (block_rows, 1), 0) + tail
    cos = cos_ref[...]
    sin = sin_ref[...]

    def window(skip):
        width = span - skip
        k = k_ref[pl.ds(start + skip, width), :]
        v = v_ref[pl.ds(start + skip, width), :]
        col = lax.broadcasted_iota(jnp.int32, (block_rows, width), 1) + skip
        visible = (col >= lo) & (col <= hi)
        for h in range(heads):
            cols = slice(h * head_dim, (h + 1) * head_dim)
            qh = q_refs[h][...].astype(jnp.float32)
            qr = (qh * cos + pltpu.roll(qh, head_dim // 2, 1) * sin).astype(jnp.bfloat16)
            s = lax.dot_general(
                qr, k, (((1,), (1,)), ((), ())), preferred_element_type=jnp.float32
            ) * scale
            s = jnp.where(visible, s, -1e30)
            m = jnp.max(s, axis=1, keepdims=True)
            p = jnp.exp(s - m)
            l = jnp.sum(p, axis=1, keepdims=True)
            o = jnp.dot(p.astype(jnp.bfloat16), v, preferred_element_type=jnp.float32)
            o_ref[0, :, cols] = (o / l).astype(o_ref.dtype)

    kmin = kmin_ref[r]

    @pl.when(kmin >= block_rows)
    def _():
        window(block_rows)

    @pl.when(kmin < block_rows)
    def _():
        window(0)


def attend(
    dest, kmin, q, table, k_arr, v_arr, lo, n_dest, head_dim, first, heads,
    first_block, blocks, key_base, prev=None, k_col=0, v_col=0,
):
    rows, all_width = q.shape
    width = heads * head_dim
    per_dev, block_rows, _ = lo.shape
    tail_blocks = (table.shape[0] - rows) // block_rows
    span = (tail_blocks + 1) * block_rows
    k_rows = k_arr.shape[0]
    kernel = functools.partial(
        attend_kernel,
        heads=heads,
        head_dim=head_dim,
        block_rows=block_rows,
        span=span,
        scale=1.0 / math.sqrt(head_dim),
        first_block=first_block,
        key_base=key_base,
        aliased=prev is not None,
    )
    flops = 4 * blocks * heads * block_rows * span * head_dim
    in_specs = [
        pl.BlockSpec((block_rows, head_dim), functools.partial(
            lambda i, dst, km, col: (i + first_block, col), col=first + head))
        for head in range(heads)
    ] + [
        pl.BlockSpec((block_rows, head_dim), lambda i, dst, km: (i + first_block + tail_blocks, 0)),
        pl.BlockSpec((block_rows, head_dim), lambda i, dst, km: (i + first_block + tail_blocks, 1)),
        pl.BlockSpec((k_rows, head_dim), lambda i, dst, km: (0, k_col)),
        pl.BlockSpec((k_rows, head_dim), lambda i, dst, km: (0, v_col)),
        pl.BlockSpec((1, block_rows, 1), lambda i, dst, km: (i + first_block, 0, 0)),
    ]
    args = [dest, kmin] + [q] * heads + [table, table, k_arr, v_arr, lo]
    aliases = {}
    if prev is not None:
        in_specs.append(pl.BlockSpec(memory_space=pl.ANY))
        args.append(prev)
        aliases = {len(args) - 1: 0}
    grid_spec = pltpu.PrefetchScalarGridSpec(
        num_scalar_prefetch=2,
        grid=(blocks,),
        in_specs=in_specs,
        out_specs=pl.BlockSpec(
            (1, block_rows, width), lambda i, dst, km: (dst[i + first_block], 0, 0)
        ),
    )
    return pl.pallas_call(
        kernel,
        grid_spec=grid_spec,
        out_shape=jax.ShapeDtypeStruct((n_dest, block_rows, width), q.dtype),
        input_output_aliases=aliases,
        cost_estimate=pl.CostEstimate(
            flops=flops,
            transcendentals=blocks * heads * block_rows * span,
            bytes_accessed=2 * blocks * block_rows * width * 2 + 2 * k_rows * head_dim * 2,
        ),
    )(*args)


def local(queries, keys, values, rope_factors, doc_lengths, owner_map):
    ctx_size = lax.axis_size("ctx")
    ctx_index = lax.axis_index("ctx")
    tp_size = lax.axis_size("tp")
    row_count = queries.shape[0]
    per_dev = owner_map.shape[1]
    block_rows = row_count // per_dev
    tail_rows = row_count // 4
    span = tail_rows + block_rows
    head_dim = 2 * rope_factors.shape[0]
    kv_heads = keys.shape[1] // head_dim
    kv_local = kv_heads // tp_size
    shard_rows = keys.shape[0]

    kv_width = kv_local * head_dim
    kv = jnp.concatenate(
        [
            keys.reshape(shard_rows, tp_size, kv_width).transpose(1, 0, 2),
            values.reshape(shard_rows, tp_size, kv_width).transpose(1, 0, 2),
        ],
        axis=2,
    )
    kv = lax.all_to_all(kv, "tp", split_axis=0, concat_axis=0, tiled=True)
    kv = kv.reshape(row_count, 2 * kv_width)
    k_own_raw = kv[:, :kv_width]
    v_own = kv[:, kv_width:]
    kv_tail = passed_along(kv[row_count - tail_rows :], "ctx", 1)

    ext_rows = row_count + tail_rows
    pos_ext = ctx_index * row_count - tail_rows + jnp.arange(ext_rows, dtype=jnp.int32)
    unused_doc, off_ext = doc_tables(doc_lengths, pos_ext)
    inverse = inverse_freqs(rope_factors, head_dim)
    table = rotation_rows(off_ext, inverse, tail_rows)
    cos_ext = table[:, :head_dim]
    sin_ext = table[:, head_dim:]

    def rotated(raw, cosine, sine):
        raw = raw.astype(jnp.float32)
        return (raw * cosine + jnp.roll(raw, head_dim // 2, axis=1) * sine).astype(jnp.bfloat16)

    k_own = rotated(k_own_raw, cos_ext[tail_rows:], sin_ext[tail_rows:])
    k_tail = rotated(kv_tail[:, :kv_width], cos_ext[:tail_rows], sin_ext[:tail_rows])
    k_ext = jnp.concatenate([k_tail, k_own], axis=0)
    v_ext = jnp.concatenate([kv_tail[:, kv_width:], v_own], axis=0)

    lo = (tail_rows + jnp.arange(row_count, dtype=jnp.int32) % block_rows - off_ext[tail_rows:])
    lo = lo.reshape(per_dev, block_rows, 1)
    kmin = lo[:, 0, 0]

    devices = jnp.arange(ctx_size, dtype=jnp.int32)
    owner_row = lax.dynamic_index_in_dim(owner_map, ctx_index, 0, keepdims=False)

    q_heads = queries.shape[1] // head_dim
    sizes = [2, 3, 3] if q_heads == 8 else [q_heads]
    tail_blocks = tail_rows // block_rows
    arrived = []
    first = 0
    for number, heads in enumerate(sizes):
        if number == 0:
            send = attend(
                owner_row, kmin, queries, table, k_own, v_own, lo, ctx_size, head_dim, first, heads,
                tail_blocks, per_dev - tail_blocks, tail_rows,
            )
            near = jnp.concatenate(
                [
                    jnp.concatenate([k_tail, kv_tail[:, kv_width:]], axis=1),
                    jnp.concatenate([k_own[:tail_rows], v_own[:tail_rows]], axis=1),
                ],
                axis=0,
            )
            send = attend(
                owner_row, kmin, queries, table, near, near, lo, ctx_size, head_dim,
                first, heads, 0, tail_blocks, 0, prev=send, k_col=0, v_col=1,
            )
        else:
            send = attend(
                owner_row, kmin, queries, table, k_ext, v_ext, lo, ctx_size, head_dim, first, heads,
                0, per_dev, 0,
            )
        arrived.append(lax.all_to_all(send, "ctx", split_axis=0, concat_axis=0, tiled=True))
        first += heads

    sources_match = owner_map == ctx_index
    my_sources = jnp.sum(
        jnp.where(sources_match, devices[:, None], 0), axis=0, dtype=jnp.int32
    )
    finished = jnp.zeros((per_dev, block_rows, queries.shape[1]), queries.dtype)
    first = 0
    for number, (heads, a) in enumerate(zip(sizes, arrived)):
        if number + 1 < len(sizes):
            finished = lax.dynamic_update_slice(
                finished, jnp.take(a, my_sources, axis=0, mode="clip"), (0, 0, first * head_dim)
            )
        else:
            for r in range(per_dev):
                piece = lax.dynamic_index_in_dim(a, my_sources[r], 0, keepdims=True)
                finished = lax.dynamic_update_slice(finished, piece, (r, 0, first * head_dim))
        first += heads
    return finished.reshape(row_count, queries.shape[1])


def solution(mesh):
    in_specs = (P("ctx", "tp"), P(("ctx", "tp"), None), P(("ctx", "tp"), None), P(), P(), P())
    out_specs = P("ctx", "tp")
    return jax.shard_map(local, mesh=mesh, in_specs=in_specs, out_specs=out_specs, check_vma=False)
```

```python
import functools
import math

import jax
import jax.numpy as jnp
from jax import lax
from jax.experimental import pallas as pl
from jax.experimental.pallas import tpu as pltpu
from jax.sharding import PartitionSpec as P

THETA = 500000.0


def passed_along(shard, axis, by):
    length = lax.axis_size(axis)
    pairs = [(i, i + by) for i in range(length) if 0 <= i + by < length]
    return lax.ppermute(shard, axis, pairs)


def doc_tables(lengths, positions):
    doc_ends = jnp.cumsum(lengths, dtype=jnp.int32)
    before = positions[:, None] >= doc_ends[None, :]
    doc_index = jnp.sum(before.astype(jnp.int32), axis=1, dtype=jnp.int32)
    doc_start = jnp.sum(jnp.where(before, lengths[None, :], 0), axis=1, dtype=jnp.int32)
    return (doc_index, positions - doc_start)


def inverse_freqs(factors, head_dim):
    half_dim = head_dim // 2
    exponent = jnp.arange(half_dim, dtype=jnp.float32) * (2.0 / head_dim)
    return 1.0 / (factors * jnp.power(jnp.float32(THETA), exponent))


def rotation_rows(offsets, inverse, distinct):
    angles = jnp.arange(distinct, dtype=jnp.int32).astype(jnp.float32)[:, None] * inverse[None, :]
    cosine = jnp.cos(angles)
    sine = jnp.sin(angles)
    table = jnp.concatenate([cosine, cosine, -sine, sine], axis=1)
    return jnp.take(table, jnp.clip(offsets, 0, distinct - 1), axis=0, mode="clip")


def rotate(vectors, offsets, inverse):
    half_dim = vectors.shape[-1] // 2
    angles = offsets.astype(jnp.float32)[:, None] * inverse[None, :]
    cosine = jnp.cos(angles)
    sine_part = jnp.sin(angles)
    first_half = vectors[..., :half_dim]
    second_half = vectors[..., half_dim:]
    return jnp.concatenate(
        [
            first_half * cosine - second_half * sine_part,
            second_half * cosine + first_half * sine_part,
        ],
        axis=-1,
    )


def attend_kernel(
    dest_ref, kmin_ref, *refs, heads, head_dim, block_rows, span, scale, first_block, key_base,
    aliased, q_inputs,
):
    q_refs = refs[:q_inputs]
    cos_ref, sin_ref, k_ref, v_ref, lo_ref = refs[q_inputs : q_inputs + 5]
    o_ref = refs[-1]
    r = pl.program_id(0) + first_block
    start = pl.multiple_of(r * block_rows - key_base, block_rows)
    tail = span - block_rows
    lo = lo_ref[0]
    hi = lax.broadcasted_iota(jnp.int32, (block_rows, 1), 0) + tail
    cos = cos_ref[...]
    sin = sin_ref[...]

    def window(skip):
        width = span - skip
        k = k_ref[pl.ds(start + skip, width), :]
        v = v_ref[pl.ds(start + skip, width), :]
        col = lax.broadcasted_iota(jnp.int32, (block_rows, width), 1) + skip
        visible = (col >= lo) & (col <= hi)
        for h in range(heads):
            cols = slice(h * head_dim, (h + 1) * head_dim)
            if q_inputs == heads:
                qh = q_refs[h][...].astype(jnp.float32)
            else:
                qh = q_refs[0][:, cols].astype(jnp.float32)
            qr = (qh * cos + pltpu.roll(qh, head_dim // 2, 1) * sin).astype(jnp.bfloat16)
            s = lax.dot_general(
                qr, k, (((1,), (1,)), ((), ())), preferred_element_type=jnp.float32
            ) * scale
            s = jnp.where(visible, s, -1e30)
            m = jnp.max(s, axis=1, keepdims=True)
            p = jnp.exp(s - m)
            l = jnp.sum(p, axis=1, keepdims=True)
            o = jnp.dot(p.astype(jnp.bfloat16), v, preferred_element_type=jnp.float32)
            o_ref[0, :, cols] = (o / l).astype(o_ref.dtype)

    kmin = kmin_ref[r]

    @pl.when(kmin >= block_rows)
    def _():
        window(block_rows)

    @pl.when(kmin < block_rows)
    def _():
        window(0)


def attend(
    dest, kmin, q, table, k_arr, v_arr, lo, n_dest, head_dim, first, heads,
    first_block, blocks, key_base, prev=None, k_col=0, v_col=0,
):
    rows, all_width = q.shape
    width = heads * head_dim
    per_dev, block_rows, _ = lo.shape
    tail_blocks = (table.shape[0] - rows) // block_rows
    span = (tail_blocks + 1) * block_rows
    k_rows = k_arr.shape[0]
    kernel = functools.partial(
        attend_kernel,
        heads=heads,
        head_dim=head_dim,
        block_rows=block_rows,
        span=span,
        scale=1.0 / math.sqrt(head_dim),
        first_block=first_block,
        key_base=key_base,
        aliased=prev is not None,
        q_inputs=1 if first % heads == 0 else heads,
    )
    flops = 4 * blocks * heads * block_rows * span * head_dim
    if first % heads == 0:
        q_specs = [pl.BlockSpec((block_rows, width), functools.partial(
            lambda i, dst, km, col: (i + first_block, col), col=first // heads))]
    else:
        q_specs = [
            pl.BlockSpec((block_rows, head_dim), functools.partial(
                lambda i, dst, km, col: (i + first_block, col), col=first + head))
            for head in range(heads)
        ]
    in_specs = q_specs + [
        pl.BlockSpec((block_rows, head_dim), lambda i, dst, km: (i + first_block + tail_blocks, 0)),
        pl.BlockSpec((block_rows, head_dim), lambda i, dst, km: (i + first_block + tail_blocks, 1)),
        pl.BlockSpec((k_rows, head_dim), lambda i, dst, km: (0, k_col)),
        pl.BlockSpec((k_rows, head_dim), lambda i, dst, km: (0, v_col)),
        pl.BlockSpec((1, block_rows, 1), lambda i, dst, km: (i + first_block, 0, 0)),
    ]
    args = [dest, kmin] + [q] * len(q_specs) + [table, table, k_arr, v_arr, lo]
    aliases = {}
    if prev is not None:
        in_specs.append(pl.BlockSpec(memory_space=pl.ANY))
        args.append(prev)
        aliases = {len(args) - 1: 0}
    grid_spec = pltpu.PrefetchScalarGridSpec(
        num_scalar_prefetch=2,
        grid=(blocks,),
        in_specs=in_specs,
        out_specs=pl.BlockSpec(
            (1, block_rows, width), lambda i, dst, km: (dst[i + first_block], 0, 0)
        ),
    )
    return pl.pallas_call(
        kernel,
        grid_spec=grid_spec,
        out_shape=jax.ShapeDtypeStruct((n_dest, block_rows, width), q.dtype),
        input_output_aliases=aliases,
        cost_estimate=pl.CostEstimate(
            flops=flops,
            transcendentals=blocks * heads * block_rows * span,
            bytes_accessed=2 * blocks * block_rows * width * 2 + 2 * k_rows * head_dim * 2,
        ),
    )(*args)


def local(queries, keys, values, rope_factors, doc_lengths, owner_map):
    ctx_size = lax.axis_size("ctx")
    ctx_index = lax.axis_index("ctx")
    tp_size = lax.axis_size("tp")
    row_count = queries.shape[0]
    per_dev = owner_map.shape[1]
    block_rows = row_count // per_dev
    tail_rows = row_count // 4
    span = tail_rows + block_rows
    head_dim = 2 * rope_factors.shape[0]
    kv_heads = keys.shape[1] // head_dim
    kv_local = kv_heads // tp_size
    shard_rows = keys.shape[0]

    kv_width = kv_local * head_dim
    kv = jnp.concatenate(
        [
            keys.reshape(shard_rows, tp_size, kv_width).transpose(1, 0, 2),
            values.reshape(shard_rows, tp_size, kv_width).transpose(1, 0, 2),
        ],
        axis=2,
    )
    kv = lax.all_to_all(kv, "tp", split_axis=0, concat_axis=0, tiled=True)
    kv = kv.reshape(row_count, 2 * kv_width)
    k_own_raw = kv[:, :kv_width]
    v_own = kv[:, kv_width:]
    kv_tail = passed_along(kv[row_count - tail_rows :], "ctx", 1)

    ext_rows = row_count + tail_rows
    pos_ext = ctx_index * row_count - tail_rows + jnp.arange(ext_rows, dtype=jnp.int32)
    unused_doc, off_ext = doc_tables(doc_lengths, pos_ext)
    inverse = inverse_freqs(rope_factors, head_dim)
    table = rotation_rows(off_ext, inverse, tail_rows)
    cos_ext = table[:, :head_dim]
    sin_ext = table[:, head_dim:]

    def rotated(raw, cosine, sine):
        raw = raw.astype(jnp.float32)
        return (raw * cosine + jnp.roll(raw, head_dim // 2, axis=1) * sine).astype(jnp.bfloat16)

    k_own = rotated(k_own_raw, cos_ext[tail_rows:], sin_ext[tail_rows:])
    k_tail = rotated(kv_tail[:, :kv_width], cos_ext[:tail_rows], sin_ext[:tail_rows])
    k_ext = jnp.concatenate([k_tail, k_own], axis=0)
    v_ext = jnp.concatenate([kv_tail[:, kv_width:], v_own], axis=0)

    lo = (tail_rows + jnp.arange(row_count, dtype=jnp.int32) % block_rows - off_ext[tail_rows:])
    lo = lo.reshape(per_dev, block_rows, 1)
    kmin = lo[:, 0, 0]

    devices = jnp.arange(ctx_size, dtype=jnp.int32)
    owner_row = lax.dynamic_index_in_dim(owner_map, ctx_index, 0, keepdims=False)

    q_heads = queries.shape[1] // head_dim
    sizes = [2, 3, 3] if q_heads == 8 else [q_heads]
    tail_blocks = tail_rows // block_rows
    arrived = []
    first = 0
    for number, heads in enumerate(sizes):
        if number == 0:
            send = attend(
                owner_row, kmin, queries, table, k_own, v_own, lo, ctx_size, head_dim, first, heads,
                tail_blocks, per_dev - tail_blocks, tail_rows,
            )
            near = jnp.concatenate(
                [
                    jnp.concatenate([k_tail, kv_tail[:, kv_width:]], axis=1),
                    jnp.concatenate([k_own[:tail_rows], v_own[:tail_rows]], axis=1),
                ],
                axis=0,
            )
            send = attend(
                owner_row, kmin, queries, table, near, near, lo, ctx_size, head_dim,
                first, heads, 0, tail_blocks, 0, prev=send, k_col=0, v_col=1,
            )
        else:
            send = attend(
                owner_row, kmin, queries, table, k_ext, v_ext, lo, ctx_size, head_dim, first, heads,
                0, per_dev, 0,
            )
        arrived.append(lax.all_to_all(send, "ctx", split_axis=0, concat_axis=0, tiled=True))
        first += heads

    sources_match = owner_map == ctx_index
    my_sources = jnp.sum(
        jnp.where(sources_match, devices[:, None], 0), axis=0, dtype=jnp.int32
    )
    finished = jnp.zeros((per_dev, block_rows, queries.shape[1]), queries.dtype)
    first = 0
    for heads, a in zip(sizes, arrived):
        finished = lax.dynamic_update_slice(
            finished, jnp.take(a, my_sources, axis=0, mode="clip"), (0, 0, first * head_dim)
        )
        first += heads
    return finished.reshape(row_count, queries.shape[1])


def solution(mesh):
    in_specs = (P("ctx", "tp"), P(("ctx", "tp"), None), P(("ctx", "tp"), None), P(), P(), P())
    out_specs = P("ctx", "tp")
    return jax.shard_map(local, mesh=mesh, in_specs=in_specs, out_specs=out_specs, check_vma=False)
```
